32 devices in a mesh: space: 8 (over y, x, core), species: 4 (over z).
Axes of the slice: x: 2, y: 2, z: 4, core: 2. Of those that a mesh axis runs over, the one named last changes fastest.
Arguments:
- cotangent: bfloat16 [4, 400, 20, 1024], P('species', None, None, 'space'), may hold values from -6 to 6
- freq: float32 [4], P('species'), may hold values from 0.2 to 0.9
- ratio: float32 [4], P('species'), may hold values from 0.5 to 1
- coupling: float32 [4, 4, 13], replicated, may hold values from 0.1 to 0.6
- wall: int32 [1024], P('space'), may hold values 0 or 1
- inlet: int32 [1024], P('space'), may hold values 0 or 1
- face_type: int32 [2, 8], P(None, 'space'), may hold values from 0 to 1
Outputs:
- grad_state: bfloat16 [4, 400, 20, 1024], P('species', None, None, 'space')
The draws below stay inside these ranges and needn't reach their ends.
Inputs may be any that keep to these rules, and one draw needn't show every extreme that they name: `wall`: 1 marks a solid cell. `inlet`: 1 marks an inlet cell. `face_type`: 0 is a specular wall, 1 a reversing wall.
All inputs are finite; a program needn't handle non-finite values. No bound on the sum of `wall` or of `inlet` on one device may be relied on, other than what follows from the above.
Results may differ from the reference program's by a relative error of at most 0.0049.
Values may be sent and summed in bfloat16 or wider, within the bound.
No kernel may reach another device: no remote copies, remote signals or barrier semaphores. Data moves between devices by JAX's collectives and lax.ppermute only.
A program may use at most 64 MiB of HBM per device.

```python
import math
import jax
import jax.numpy as jnp
from jax import lax

SPECIES = 4
NODES = 20
MOMENTS = 13
NZ = 128
PAIRS = 400
NX = 8
CELLS = 1024


def plant(entries, rng, least, high):
    longest = entries.shape.index(max(entries.shape))
    spots = []
    for shift in (0, 1):
        where = [jax.random.randint(jax.random.fold_in(rng, axis), (), 0, length) for axis, length in enumerate(entries.shape)]
        where[longest] = (where[longest] + shift) % entries.shape[longest]
        spots.append(tuple(where))
    return entries.at[spots[0]].set(least).at[spots[1]].set(high)


def level_of(rng, extent, split, low, top_value):
    def one(axis_at, shards_of):
        steps = jax.random.uniform(jax.random.fold_in(jax.random.fold_in(rng, 6), axis_at), (shards_of,), jnp.float32, low / len(split), top_value / len(split))
        return jnp.repeat(jnp.exp(steps), extent[axis_at] // shards_of).reshape((-1,) + (1,) * (len(extent) - axis_at - 1))

    factor_of = one(*split[0])
    for cut in split[1:]:
        factor_of = factor_of * one(*cut)
    return factor_of


def bell_draw(rng, dims, width, most, pieces=(), held_as=jnp.bfloat16):
    loudness = level_of(rng, dims, pieces, -0.22, 0.18) if pieces else 1.0
    array = jax.random.normal(rng, dims, jnp.float32) * width * loudness
    return jnp.minimum(jnp.maximum(array, -most), most).astype(held_as)


def setup_inputs(seed: int = 0) -> dict:
    keys = jax.random.split(jax.random.key(seed), 8)
    return {
        "cotangent": bell_draw(keys[0], (SPECIES, PAIRS, NODES, CELLS), 1.0, 6.0, ((0, 4), (3, 8))),
        "freq": jnp.clip(jnp.exp(math.log(0.9) - 1.50407736 * jax.random.uniform(keys[1], (SPECIES,), jnp.float32) ** level_of(keys[1], (SPECIES,), ((0, 4),), -0.2, 0.2)), 0.2, 0.9),
        "ratio": jnp.clip(0.5 + 0.5 * jax.random.uniform(keys[2], (SPECIES,), jnp.float32) ** level_of(keys[2], (SPECIES,), ((0, 4),), -0.2, 0.2), 0.5, 1.0),
        "coupling": jnp.clip(jax.random.uniform(keys[3], (SPECIES, SPECIES, MOMENTS), jnp.float32, 0.1, 0.6), 0.1, 0.6),
        "wall": plant((jax.random.randint(keys[4], (CELLS,), 0, 8) < 1).astype(jnp.int32), jax.random.fold_in(keys[4], 1), 0, 1),
        "inlet": plant((jax.random.randint(keys[5], (CELLS,), 0, 8) < 1).astype(jnp.int32), jax.random.fold_in(keys[5], 1), 0, 1),
        "face_type": plant(jax.random.randint(keys[6], (2, NX), 0, 2), jax.random.fold_in(keys[6], 1), 0, 1).astype(jnp.int32),
    }


courant_max = 0.45
node_reach = 2.85

def velocity_tables(node_count):
    pair_count = node_count * node_count
    spacing = 2.0 * node_reach / (node_count - 1)
    node_line = (jnp.arange(node_count, dtype=jnp.int32).astype(jnp.float32) - 0.5 * (node_count - 1)) * spacing
    grid_shape = (pair_count, node_count)
    along_x = jnp.broadcast_to(jnp.repeat(node_line, node_count)[:, None], grid_shape)
    along_y = jnp.broadcast_to(jnp.tile(node_line, node_count)[:, None], grid_shape)
    along_z = jnp.broadcast_to(node_line[None, :], grid_shape)
    square = along_x * along_x + along_y * along_y + along_z * along_z
    heat_term = square - 2.5
    functions = [jnp.ones(grid_shape, jnp.float32), along_x, along_y, along_z, square - 1.5, along_x * along_y, along_x * along_z, along_y * along_z, along_x * along_x - along_y * along_y, along_y * along_y - along_z * along_z, along_x * heat_term, along_y * heat_term, along_z * heat_term]
    stacked = jnp.stack(functions).reshape(len(functions), pair_count * node_count)
    basis_table = stacked / jnp.sqrt(lax.optimization_barrier(jnp.mean(stacked * stacked, axis=1, keepdims=True)))
    weights = jnp.exp(-square).reshape(-1) * (spacing * spacing * spacing) / math.pi ** 1.5
    recon_table = basis_table * weights[None, :]
    return (node_line, basis_table, recon_table)

def keep_factor(wall, inlet, pair_count):
    upward = (jnp.arange(pair_count, dtype=jnp.int32) >= pair_count // 2).astype(jnp.float32)
    open_cells = (1 - wall).astype(jnp.float32)
    inflow = inlet.astype(jnp.float32)
    return open_cells[None, None, :] * (1.0 - upward[:, None, None] * inflow[None, None, :])

def reference(cotangent, freq, ratio, coupling, wall, inlet, face_type):
    species_count, pair_count, node_count, cell_count = cotangent.shape
    node_line, basis_table, recon_table = velocity_tables(node_count)
    keep_mask = keep_factor(wall, inlet, pair_count)

    def moments_of(slab):
        masked = slab.astype(jnp.float32) * keep_mask
        return jnp.dot(basis_table, masked.reshape(pair_count * node_count, cell_count), precision=lax.Precision.HIGHEST, preferred_element_type=jnp.float32)
    moments = lax.map(moments_of, cotangent)
    pair_x = jnp.repeat(node_line, node_count)

    def adjoint_of(items):
        slab, rate_value, speed_value, row_k = items
        masked = slab.astype(jnp.float32) * keep_mask
        cross_terms = lax.optimization_barrier(jnp.sum(row_k[:, :, None] * moments, axis=0))
        rebuilt = jnp.dot(recon_table.T, cross_terms, precision=lax.Precision.HIGHEST, preferred_element_type=jnp.float32).reshape(pair_count, node_count, cell_count)
        relaxed = ((1.0 - rate_value) * masked + rebuilt).astype(jnp.bfloat16)
        field = relaxed.astype(jnp.float32).reshape(pair_count, node_count, NX, NZ)
        scale_factor = courant_max * speed_value / node_reach
        adv_x = (scale_factor * pair_x)[:, None, None, None]
        adv_z = (scale_factor * node_line)[None, :, None, None]
        plus_x = jnp.maximum(adv_x, 0.0)
        minus_x = jnp.maximum(-adv_x, 0.0)
        plus_z = jnp.maximum(adv_z, 0.0)
        minus_z = jnp.maximum(-adv_z, 0.0)
        zero_plane = jnp.zeros_like(field[..., :1])
        upper_z = jnp.concatenate([field[..., 1:], zero_plane], axis=3)
        lower_z = jnp.concatenate([zero_plane, field[..., :-1]], axis=3)
        result = (1.0 - jnp.abs(adv_x) - jnp.abs(adv_z)) * field
        result = result + plus_x * jnp.roll(field, -1, axis=2) + minus_x * jnp.roll(field, 1, axis=2)
        result = result + plus_z * upper_z + minus_z * lower_z
        bottom_part = plus_z[..., 0] * field[..., 0]
        bottom_add = jnp.where(face_type[0][None, None, :] == 1, jnp.flip(bottom_part, axis=(0, 1)), jnp.flip(bottom_part, axis=1))
        top_part = minus_z[..., 0] * field[..., NZ - 1]
        top_add = jnp.where(face_type[1][None, None, :] == 1, jnp.flip(top_part, axis=(0, 1)), jnp.flip(top_part, axis=1))
        result = result.at[..., 0].add(bottom_add)
        result = result.at[..., NZ - 1].add(top_add)
        return result.reshape(pair_count, node_count, cell_count).astype(jnp.bfloat16)
    return lax.map(adjoint_of, (cotangent, freq, ratio, coupling))
```

```python
import math

import numpy as np
import jax
import jax.numpy as jnp
from jax import lax
from jax.sharding import PartitionSpec as P

NZ = 128

courant_max = 0.45
node_reach = 2.85


def passed_along(value, axis, steps):
    count = lax.axis_size(axis)
    pairs = [(source, (source + steps) % count) for source in range(count)]
    return lax.ppermute(value, axis, pairs)


def velocity_tables(node_count):
    pair_count = node_count * node_count
    spacing = 2.0 * node_reach / (node_count - 1)
    node_line = (np.arange(node_count, dtype=np.float64) - 0.5 * (node_count - 1)) * spacing
    grid_shape = (pair_count, node_count)
    along_x = np.broadcast_to(np.repeat(node_line, node_count)[:, None], grid_shape)
    along_y = np.broadcast_to(np.tile(node_line, node_count)[:, None], grid_shape)
    along_z = np.broadcast_to(node_line[None, :], grid_shape)
    square = along_x * along_x + along_y * along_y + along_z * along_z
    heat_term = square - 2.5
    functions = [
        np.ones(grid_shape),
        along_x,
        along_y,
        along_z,
        square - 1.5,
        along_x * along_y,
        along_x * along_z,
        along_y * along_z,
        along_x * along_x - along_y * along_y,
        along_y * along_y - along_z * along_z,
        along_x * heat_term,
        along_y * heat_term,
        along_z * heat_term,
    ]
    stacked = np.stack(functions)
    basis = stacked / np.sqrt(np.mean(stacked * stacked, axis=(1, 2), keepdims=True))
    weights = np.exp(-square) * (spacing * spacing * spacing) / math.pi**1.5
    recon = basis * weights[None]
    return node_line, basis, recon


def bf16_split(table, parts):
    rest = np.asarray(table, np.float64)
    pieces = []
    for _ in range(parts):
        piece = rest.astype(np.float32).astype(jnp.bfloat16).astype(np.float64)
        pieces.append(piece)
        rest = rest - piece
    return pieces


def on_device(cotangent, freq, ratio, coupling, wall, inlet, face_type):
    pair_count = cotangent.shape[1]
    node_count = cotangent.shape[2]
    cell_count = cotangent.shape[3]
    assert cell_count == NZ
    half = pair_count // 2
    moment_count = coupling.shape[2]
    species_count = lax.axis_size("species")

    node_line, basis, recon = velocity_tables(node_count)
    basis_k = np.transpose(basis, (0, 2, 1)).reshape(moment_count, node_count * pair_count)
    basis_parts = np.concatenate(bf16_split(basis_k, 3), axis=0)
    basis_parts = jnp.asarray(basis_parts.astype(jnp.bfloat16))
    recon_k = np.transpose(recon, (0, 2, 1)).astype(np.float32)

    field_in = jnp.transpose(cotangent[0], (1, 0, 2))
    upper_in = field_in[:, half:, :]
    lower_in = field_in[:, :half, :]
    got_next = passed_along(upper_in, "space", -1)
    got_prev = passed_along(lower_in, "space", 1)

    open_cells = (1 - wall).astype(jnp.float32)
    keep_upper = open_cells * (1.0 - inlet.astype(jnp.float32))
    upward = (jnp.arange(pair_count) >= half)[None, :, None]
    keep = jnp.where(upward, keep_upper[None, None, :], open_cells[None, None, :])
    masked = field_in * keep.astype(jnp.bfloat16)
    parts = jnp.dot(
        basis_parts,
        masked.reshape(node_count * pair_count, cell_count),
        preferred_element_type=jnp.float32,
    )
    moments = parts[:moment_count] + parts[moment_count : 2 * moment_count] + parts[2 * moment_count :]

    species_index = lax.axis_index("species")
    row_k = lax.dynamic_index_in_dim(coupling, species_index, axis=0, keepdims=False)
    own_weight = lax.dynamic_index_in_dim(row_k, species_index, axis=0, keepdims=False)
    cross = own_weight[:, None] * moments
    for shift in range(1, species_count):
        source = (species_index - shift) % species_count
        other = passed_along(moments, "species", shift)
        weight = lax.dynamic_index_in_dim(row_k, source, axis=0, keepdims=False)
        cross = cross + weight[:, None] * other

    packet = jnp.concatenate([cross, open_cells[None], keep_upper[None]], axis=0)
    packet_next = passed_along(packet, "space", -1)
    packet_prev = passed_along(packet, "space", 1)

    rate_value = freq[0]
    recon_all = lax.optimization_barrier(jnp.asarray(recon_k))

    def relaxed_of(values, keep_rows, cross_rows, recon_rows):
        rebuilt = jnp.einsum(
            "mnp,mc->npc",
            recon_rows,
            cross_rows,
            precision=lax.Precision.HIGHEST,
            preferred_element_type=jnp.float32,
        )
        return ((1.0 - rate_value) * (values.astype(jnp.float32) * keep_rows) + rebuilt).astype(
            jnp.bfloat16
        ).astype(jnp.float32)

    relaxed = relaxed_of(masked, 1.0, cross, recon_all)
    relaxed_next = relaxed_of(
        got_next,
        packet_next[moment_count + 1][None, None, :],
        packet_next[:moment_count],
        recon_all[:, :, half:],
    )
    relaxed_prev = relaxed_of(
        got_prev,
        packet_prev[moment_count][None, None, :],
        packet_prev[:moment_count],
        recon_all[:, :, :half],
    )

    scale_factor = courant_max * ratio[0] / node_reach
    line = jnp.asarray(node_line.astype(np.float32))
    adv_x = (scale_factor * jnp.repeat(line, node_count))[None, :, None]
    adv_z = (scale_factor * line)[:, None, None]
    plus_x = jnp.maximum(adv_x, 0.0)
    minus_x = jnp.maximum(-adv_x, 0.0)
    plus_z = jnp.maximum(adv_z, 0.0)
    minus_z = jnp.maximum(-adv_z, 0.0)

    shifted_x = jnp.concatenate(
        [minus_x[:, :half] * relaxed_prev, plus_x[:, half:] * relaxed_next], axis=1
    )
    zero_plane = jnp.zeros_like(relaxed[..., :1])
    upper_z = jnp.concatenate([relaxed[..., 1:], zero_plane], axis=2)
    lower_z = jnp.concatenate([zero_plane, relaxed[..., :-1]], axis=2)

    bottom_part = plus_z[::-1, :, 0] * relaxed[::-1, :, 0]
    bottom_add = jnp.where(face_type[0, 0] == 1, bottom_part[:, ::-1], bottom_part)
    top_part = minus_z[::-1, :, 0] * relaxed[::-1, :, NZ - 1]
    top_add = jnp.where(face_type[1, 0] == 1, top_part[:, ::-1], top_part)
    lane = lax.broadcasted_iota(jnp.int32, (1, 1, cell_count), 2)

    result = (1.0 - jnp.abs(adv_x) - jnp.abs(adv_z)) * relaxed
    result = result + shifted_x
    result = result + plus_z * upper_z + minus_z * lower_z
    result = result + jnp.where(lane == 0, bottom_add[:, :, None], 0.0)
    result = result + jnp.where(lane == NZ - 1, top_add[:, :, None], 0.0)
    out = result.astype(jnp.bfloat16)
    return jnp.transpose(out, (1, 0, 2))[None]


def solution(mesh):
    in_specs = (
        P("species", None, None, "space"),
        P("species"),
        P("species"),
        P(),
        P("space"),
        P("space"),
        P(None, "space"),
    )
    out_specs = P("species", None, None, "space")
    return jax.shard_map(
        on_device, mesh=mesh, in_specs=in_specs, out_specs=out_specs, check_vma=False
    )
```

```python
import math

import numpy as np
import jax
import jax.numpy as jnp
from jax import lax
from jax.experimental import pallas as pl
from jax.experimental.pallas import tpu as pltpu
from jax.sharding import PartitionSpec as P

NZ = 128

courant_max = 0.45
node_reach = 2.85


def passed_along(value, axis, steps):
    count = lax.axis_size(axis)
    pairs = [(source, (source + steps) % count) for source in range(count)]
    return lax.ppermute(value, axis, pairs)


def velocity_tables(node_count):
    pair_count = node_count * node_count
    spacing = 2.0 * node_reach / (node_count - 1)
    node_line = (np.arange(node_count, dtype=np.float64) - 0.5 * (node_count - 1)) * spacing
    grid_shape = (pair_count, node_count)
    along_x = np.broadcast_to(np.repeat(node_line, node_count)[:, None], grid_shape)
    along_y = np.broadcast_to(np.tile(node_line, node_count)[:, None], grid_shape)
    along_z = np.broadcast_to(node_line[None, :], grid_shape)
    square = along_x * along_x + along_y * along_y + along_z * along_z
    heat_term = square - 2.5
    functions = [
        np.ones(grid_shape),
        along_x,
        along_y,
        along_z,
        square - 1.5,
        along_x * along_y,
        along_x * along_z,
        along_y * along_z,
        along_x * along_x - along_y * along_y,
        along_y * along_y - along_z * along_z,
        along_x * heat_term,
        along_y * heat_term,
        along_z * heat_term,
    ]
    stacked = np.stack(functions)
    basis = stacked / np.sqrt(np.mean(stacked * stacked, axis=(1, 2), keepdims=True))
    weights = np.exp(-square) * (spacing * spacing * spacing) / math.pi**1.5
    recon = basis * weights[None]
    return node_line, basis, recon


def bf16_split(table, parts):
    rest = np.asarray(table, np.float64)
    pieces = []
    for _ in range(parts):
        piece = rest.astype(np.float32).astype(jnp.bfloat16).astype(np.float64)
        pieces.append(piece)
        rest = rest - piece
    return pieces


def on_device(cotangent, freq, ratio, coupling, wall, inlet, face_type):
    pair_count = cotangent.shape[1]
    node_count = cotangent.shape[2]
    cell_count = cotangent.shape[3]
    assert cell_count == NZ
    half = pair_count // 2
    moment_count = coupling.shape[2]
    species_count = lax.axis_size("species")

    node_line, basis, recon = velocity_tables(node_count)
    basis_k = np.transpose(basis, (0, 2, 1)).reshape(moment_count, node_count * pair_count)
    basis_parts = np.concatenate(bf16_split(basis_k, 3), axis=0)
    basis_parts = jnp.asarray(basis_parts.astype(jnp.bfloat16))
    weight_k = (recon[0] / basis[0]).T.reshape(-1).astype(np.float32)

    field_in = jnp.transpose(cotangent[0], (1, 0, 2))
    upper_in = field_in[:, half:, :]
    lower_in = field_in[:, :half, :]
    got_next = passed_along(upper_in, "space", -1)
    got_prev = passed_along(lower_in, "space", 1)

    open_cells = (1 - wall).astype(jnp.float32)
    keep_upper = open_cells * (1.0 - inlet.astype(jnp.float32))
    upward = (jnp.arange(pair_count) >= half)[None, :, None]
    keep = jnp.where(upward, keep_upper[None, None, :], open_cells[None, None, :])
    masked = field_in * keep.astype(jnp.bfloat16)
    parts = jnp.dot(
        basis_parts,
        masked.reshape(node_count * pair_count, cell_count),
        preferred_element_type=jnp.float32,
    )
    moments = parts[:moment_count] + parts[moment_count : 2 * moment_count] + parts[2 * moment_count :]

    species_index = lax.axis_index("species")
    row_k = lax.dynamic_index_in_dim(coupling, species_index, axis=0, keepdims=False)
    own_weight = lax.dynamic_index_in_dim(row_k, species_index, axis=0, keepdims=False)
    cross = own_weight[:, None] * moments
    for shift in range(1, species_count):
        source = (species_index - shift) % species_count
        other = passed_along(moments, "species", shift)
        weight = lax.dynamic_index_in_dim(row_k, source, axis=0, keepdims=False)
        cross = cross + weight[:, None] * other

    packet = jnp.concatenate([cross, open_cells[None], keep_upper[None]], axis=0)
    packet_next = passed_along(packet, "space", -1)
    packet_prev = passed_along(packet, "space", 1)

    rate_value = freq[0]
    scale_factor = courant_max * ratio[0] / node_reach
    line = jnp.asarray(node_line.astype(np.float32))
    pair_line = jnp.repeat(line, node_count)
    adv_x = jnp.abs(scale_factor * pair_line)
    adv_z = jnp.abs(scale_factor * line)
    columns = jnp.broadcast_to(
        jnp.stack([1.0 - adv_x, adv_x])[:, :, None], (2, pair_count, cell_count)
    )
    keep_rows = (1.0 - rate_value) * jnp.stack(
        [open_cells, keep_upper, packet_next[moment_count + 1], packet_prev[moment_count]]
    )
    keep_rows = jnp.concatenate([keep_rows, jnp.zeros((4, cell_count), jnp.float32)], axis=0)

    basis_run = lax.optimization_barrier(basis_parts).astype(jnp.float32)
    basis_sum = (
        basis_run[:moment_count] + basis_run[moment_count : 2 * moment_count]
    ) + basis_run[2 * moment_count :]
    recon_all = (basis_sum * jnp.asarray(weight_k)[None]).reshape(moment_count, node_count, pair_count)
    r1 = recon_all.astype(jnp.bfloat16)
    rest = recon_all - r1.astype(jnp.float32)
    r2 = rest.astype(jnp.bfloat16)
    r3 = (rest - r2.astype(jnp.float32)).astype(jnp.bfloat16)
    lanes = 128
    filler = jnp.zeros((lanes - 6 * moment_count, node_count, pair_count), jnp.bfloat16)
    recon_parts = jnp.transpose(
        jnp.concatenate([r1, r1, r2, r1, r2, r3, filler], axis=0), (1, 2, 0)
    )

    def cross_parts(rows):
        c1 = rows.astype(jnp.bfloat16)
        left = rows - c1.astype(jnp.float32)
        c2 = left.astype(jnp.bfloat16)
        c3 = (left - c2.astype(jnp.float32)).astype(jnp.bfloat16)
        pad = jnp.zeros((lanes - 6 * moment_count, cell_count), jnp.bfloat16)
        return jnp.concatenate([c1, c2, c1, c3, c2, c1, pad], axis=0)

    cross_mats = jnp.stack(
        [cross_parts(cross), cross_parts(packet_next[:moment_count]), cross_parts(packet_prev[:moment_count])]
    )
    flip_rows = lax.broadcasted_iota(jnp.int32, (pair_count, pair_count), 0)
    flip_cols = lax.broadcasted_iota(jnp.int32, (pair_count, pair_count), 1)
    flip = (flip_rows + flip_cols == pair_count - 1).astype(jnp.bfloat16)
    z_weights = jnp.concatenate([adv_z, jnp.zeros((32 - node_count,), jnp.float32)])
    faces = face_type[:, 0]

    out_lower, out_upper = advect_kernel(
        field_in, got_next, got_prev, recon_parts, cross_mats, keep_rows, columns, flip, z_weights, faces
    )
    out = jnp.concatenate([out_lower, out_upper], axis=0)
    return jnp.transpose(out, (1, 0, 2))[None]


def advect_kernel(field_in, got_next, got_prev, recon_parts, cross_mats, keep_rows, columns, flip, z_weights, faces):
    node_count, pair_count, cell_count = field_in.shape
    half = pair_count // 2
    steps = node_count // 2

    def kernel(zw_ref, face_ref, cot_a, cot_b, nxt_a, nxt_b, prv_a, prv_b, rec_a, rec_b,
               cm_ref, kr_ref, col_ref, flip_ref, out_a, out_b):
        j = pl.program_id(0)
        row = lax.broadcasted_iota(jnp.int32, (pair_count, cell_count), 0)
        lane = lax.broadcasted_iota(jnp.int32, (pair_count, cell_count), 1)
        kr = kr_ref[...]
        keep = jnp.where(row >= half, kr[1:2, :], kr[0:1, :])
        own = cm_ref[0]
        nxt_m = cm_ref[1]
        prv_m = cm_ref[2]

        def relax(values, rec, mat, keep_factor):
            rebuilt = jnp.dot(rec, mat, preferred_element_type=jnp.float32)
            return (keep_factor * values.astype(jnp.float32) + rebuilt).astype(jnp.bfloat16)

        def halo(nxt, prv, rec):
            up = jnp.dot(rec, nxt_m, preferred_element_type=jnp.float32)[half:]
            down = jnp.dot(rec, prv_m, preferred_element_type=jnp.float32)[:half]
            up = (kr[2:3, :] * nxt.astype(jnp.float32) + up).astype(jnp.bfloat16)
            down = (kr[3:4, :] * prv.astype(jnp.float32) + down).astype(jnp.bfloat16)
            return jnp.concatenate([down.astype(jnp.float32), up.astype(jnp.float32)], axis=0)

        rec_a_v = rec_a[0]
        rec_b_v = rec_b[0]
        relaxed_a = relax(cot_a[0], rec_a_v, own, keep)
        relaxed_b = relax(cot_b[0], rec_b_v, own, keep)
        edges = jnp.where(lane == 0, relaxed_b, relaxed_a)
        flipped = jnp.dot(flip_ref[...], edges, preferred_element_type=jnp.float32)
        edges32 = edges.astype(jnp.float32)
        source_a = jnp.where(face_ref[0] == 1, flipped, edges32)
        source_b = jnp.where(face_ref[1] == 1, flipped, edges32)
        ra = relaxed_a.astype(jnp.float32)
        rb = relaxed_b.astype(jnp.float32)
        near_a = jnp.where(lane == 0, source_a, pltpu.roll(ra, 1, 1))
        near_b = jnp.where(lane == cell_count - 1, source_b, pltpu.roll(rb, cell_count - 1, 1))
        base = col_ref[0]
        side = col_ref[1]
        zw_a = zw_ref[j]
        zw_b = zw_ref[node_count - 1 - j]
        halo_a = halo(nxt_a[0], prv_a[0], rec_a_v)
        halo_b = halo(nxt_b[0], prv_b[0], rec_b_v)
        res_a = (base - zw_a) * ra + side * halo_a
        res_a = res_a + zw_a * near_a
        res_b = (base - zw_b) * rb + side * halo_b
        res_b = res_b + zw_b * near_b
        out_a[0] = res_a.astype(jnp.bfloat16)
        out_b[0] = res_b.astype(jnp.bfloat16)

    lower = lambda j: (j, 0, 0)
    upper = lambda j: (node_count - 1 - j, 0, 0)
    fixed3 = lambda j: (0, 0, 0)
    fixed2 = lambda j: (0, 0)
    slab = (1, pair_count, cell_count)
    halo_slab = (1, half, cell_count)
    smem = pl.BlockSpec(memory_space=pltpu.SMEM)
    in_specs = [
        smem,
        smem,
        pl.BlockSpec(slab, lower),
        pl.BlockSpec(slab, upper),
        pl.BlockSpec(halo_slab, lower),
        pl.BlockSpec(halo_slab, upper),
        pl.BlockSpec(halo_slab, lower),
        pl.BlockSpec(halo_slab, upper),
        pl.BlockSpec(slab, lower),
        pl.BlockSpec(slab, upper),
        pl.BlockSpec(cross_mats.shape, fixed3),
        pl.BlockSpec(keep_rows.shape, fixed2),
        pl.BlockSpec(columns.shape, fixed3),
        pl.BlockSpec(flip.shape, fixed2),
    ]
    out_specs = [
        pl.BlockSpec(slab, lambda j: (j, 0, 0)),
        pl.BlockSpec(slab, lambda j: (steps - 1 - j, 0, 0)),
    ]
    out_shape = [
        jax.ShapeDtypeStruct((steps, pair_count, cell_count), jnp.bfloat16),
        jax.ShapeDtypeStruct((node_count - steps, pair_count, cell_count), jnp.bfloat16),
    ]
    return pl.pallas_call(
        kernel,
        grid=(steps,),
        in_specs=in_specs,
        out_specs=out_specs,
        out_shape=out_shape,
    )(z_weights, faces, field_in, field_in, got_next, got_next, got_prev, got_prev,
      recon_parts, recon_parts, cross_mats, keep_rows, columns, flip)


def solution(mesh):
    in_specs = (
        P("species", None, None, "space"),
        P("species"),
        P("species"),
        P(),
        P("space"),
        P("space"),
        P(None, "space"),
    )
    out_specs = P("species", None, None, "space")
    return jax.shard_map(
        on_device, mesh=mesh, in_specs=in_specs, out_specs=out_specs, check_vma=False
    )
```

```python
import math

import numpy as np
import jax
import jax.numpy as jnp
from jax import lax
from jax.experimental import pallas as pl
from jax.experimental.pallas import tpu as pltpu
from jax.sharding import PartitionSpec as P

NZ = 128

courant_max = 0.45
node_reach = 2.85


def passed_along(value, axis, steps):
    count = lax.axis_size(axis)
    pairs = [(source, (source + steps) % count) for source in range(count)]
    return lax.ppermute(value, axis, pairs)


def velocity_tables(node_count):
    pair_count = node_count * node_count
    spacing = 2.0 * node_reach / (node_count - 1)
    node_line = (np.arange(node_count, dtype=np.float64) - 0.5 * (node_count - 1)) * spacing
    grid_shape = (pair_count, node_count)
    along_x = np.broadcast_to(np.repeat(node_line, node_count)[:, None], grid_shape)
    along_y = np.broadcast_to(np.tile(node_line, node_count)[:, None], grid_shape)
    along_z = np.broadcast_to(node_line[None, :], grid_shape)
    square = along_x * along_x + along_y * along_y + along_z * along_z
    heat_term = square - 2.5
    functions = [
        np.ones(grid_shape),
        along_x,
        along_y,
        along_z,
        square - 1.5,
        along_x * along_y,
        along_x * along_z,
        along_y * along_z,
        along_x * along_x - along_y * along_y,
        along_y * along_y - along_z * along_z,
        along_x * heat_term,
        along_y * heat_term,
        along_z * heat_term,
    ]
    stacked = np.stack(functions)
    basis = stacked / np.sqrt(np.mean(stacked * stacked, axis=(1, 2), keepdims=True))
    weights = np.exp(-square) * (spacing * spacing * spacing) / math.pi**1.5
    recon = basis * weights[None]
    return node_line, basis, recon


def bf16_split(table, parts):
    rest = np.asarray(table, np.float64)
    pieces = []
    for _ in range(parts):
        piece = rest.astype(np.float32).astype(jnp.bfloat16).astype(np.float64)
        pieces.append(piece)
        rest = rest - piece
    return pieces


def on_device(cotangent, freq, ratio, coupling, wall, inlet, face_type):
    pair_count = cotangent.shape[1]
    node_count = cotangent.shape[2]
    cell_count = cotangent.shape[3]
    assert cell_count == NZ
    half = pair_count // 2
    moment_count = coupling.shape[2]
    species_count = lax.axis_size("species")

    node_line, basis, recon = velocity_tables(node_count)
    basis_k = np.transpose(basis, (0, 2, 1)).reshape(moment_count, node_count * pair_count)
    basis_parts = np.concatenate(bf16_split(basis_k, 3), axis=0)
    basis_parts = jnp.asarray(basis_parts.astype(jnp.bfloat16))
    weight_k = (recon[0] / basis[0]).T.reshape(-1).astype(np.float32)

    field_in = jnp.transpose(cotangent[0], (1, 0, 2))
    upper_in = field_in[:, half:, :]
    lower_in = field_in[:, :half, :]
    got_next = passed_along(upper_in, "space", -1)
    got_prev = passed_along(lower_in, "space", 1)

    open_cells = (1 - wall).astype(jnp.float32)
    keep_upper = open_cells * (1.0 - inlet.astype(jnp.float32))
    upward = (jnp.arange(pair_count) >= half)[None, :, None]
    keep = jnp.where(upward, keep_upper[None, None, :], open_cells[None, None, :])
    masked = field_in * keep.astype(jnp.bfloat16)
    parts = jnp.dot(
        basis_parts,
        masked.reshape(node_count * pair_count, cell_count),
        preferred_element_type=jnp.float32,
    )
    moments = parts[:moment_count] + parts[moment_count : 2 * moment_count] + parts[2 * moment_count :]

    species_index = lax.axis_index("species")
    row_k = lax.dynamic_index_in_dim(coupling, species_index, axis=0, keepdims=False)
    own_weight = lax.dynamic_index_in_dim(row_k, species_index, axis=0, keepdims=False)
    cross = own_weight[:, None] * moments
    for shift in range(1, species_count):
        source = (species_index - shift) % species_count
        other = passed_along(moments, "species", shift)
        weight = lax.dynamic_index_in_dim(row_k, source, axis=0, keepdims=False)
        cross = cross + weight[:, None] * other

    packet = jnp.concatenate([cross, open_cells[None], keep_upper[None]], axis=0)
    packet_next = passed_along(packet, "space", -1)
    packet_prev = passed_along(packet, "space", 1)

    rate_value = freq[0]
    scale_factor = courant_max * ratio[0] / node_reach
    line = jnp.asarray(node_line.astype(np.float32))
    pair_line = jnp.repeat(line, node_count)
    adv_x = jnp.abs(scale_factor * pair_line)
    adv_z = jnp.abs(scale_factor * line)
    columns = jnp.broadcast_to(
        jnp.stack([1.0 - adv_x, adv_x])[:, :, None], (2, pair_count, cell_count)
    )
    keep_rows = (1.0 - rate_value) * jnp.stack(
        [open_cells, keep_upper, packet_next[moment_count + 1], packet_prev[moment_count]]
    )
    keep_rows = jnp.concatenate([keep_rows, jnp.zeros((4, cell_count), jnp.float32)], axis=0)

    basis_run = lax.optimization_barrier(basis_parts).astype(jnp.float32)
    basis_sum = (
        basis_run[:moment_count] + basis_run[moment_count : 2 * moment_count]
    ) + basis_run[2 * moment_count :]
    recon_all = (basis_sum * jnp.asarray(weight_k)[None]).reshape(moment_count, node_count, pair_count)
    r1 = recon_all.astype(jnp.bfloat16)
    rest = recon_all - r1.astype(jnp.float32)
    r2 = rest.astype(jnp.bfloat16)
    r3 = (rest - r2.astype(jnp.float32)).astype(jnp.bfloat16)
    lanes = 128
    order = [0, 0, 1, 0, 1, 2]
    place = np.zeros((3 * moment_count, lanes), np.float32)
    for block, part in enumerate(order):
        for m in range(moment_count):
            place[part * moment_count + m, block * moment_count + m] = 1.0
    stacked_parts = jnp.concatenate([r1, r2, r3], axis=0).reshape(3 * moment_count, node_count * pair_count)
    recon_parts = lax.dot_general(
        stacked_parts,
        jnp.asarray(place, jnp.bfloat16),
        (((0,), (0,)), ((), ())),
        preferred_element_type=jnp.float32,
    ).astype(jnp.bfloat16).reshape(node_count, pair_count, lanes)

    def cross_parts(rows):
        c1 = rows.astype(jnp.bfloat16)
        left = rows - c1.astype(jnp.float32)
        c2 = left.astype(jnp.bfloat16)
        c3 = (left - c2.astype(jnp.float32)).astype(jnp.bfloat16)
        pad = jnp.zeros((lanes - 6 * moment_count, cell_count), jnp.bfloat16)
        return jnp.concatenate([c1, c2, c1, c3, c2, c1, pad], axis=0)

    cross_mats = jnp.stack(
        [cross_parts(cross), cross_parts(packet_next[:moment_count]), cross_parts(packet_prev[:moment_count])]
    )
    flip_rows = lax.broadcasted_iota(jnp.int32, (pair_count, pair_count), 0)
    flip_cols = lax.broadcasted_iota(jnp.int32, (pair_count, pair_count), 1)
    flip = (flip_rows + flip_cols == pair_count - 1).astype(jnp.bfloat16)
    z_weights = jnp.concatenate([adv_z, jnp.zeros((32 - node_count,), jnp.float32)])
    faces = face_type[:, 0]

    out = advect_kernel(
        field_in, got_next, got_prev, recon_parts, cross_mats, keep_rows, columns, flip, z_weights, faces
    )
    return jnp.transpose(out, (1, 0, 2))[None]


def advect_kernel(field_in, got_next, got_prev, recon_parts, cross_mats, keep_rows, columns, flip, z_weights, faces):
    node_count, pair_count, cell_count = field_in.shape
    half = pair_count // 2
    steps = node_count // 2

    def kernel(zw_ref, face_ref, cot_a, cot_b, nxt_a, nxt_b, prv_a, prv_b, rec_a, rec_b,
               cm_ref, kr_ref, col_ref, flip_ref, out_hbm, slots, sems):
        j = pl.program_id(0)
        slot = j % 2

        def copies(step, at):
            return (
                pltpu.make_async_copy(slots.at[at, 0], out_hbm.at[step], sems.at[at, 0]),
                pltpu.make_async_copy(slots.at[at, 1], out_hbm.at[node_count - 1 - step], sems.at[at, 1]),
            )

        @pl.when(j >= 2)
        def _():
            for copy in copies(j - 2, slot):
                copy.wait()

        row = lax.broadcasted_iota(jnp.int32, (pair_count, cell_count), 0)
        lane = lax.broadcasted_iota(jnp.int32, (pair_count, cell_count), 1)
        kr = kr_ref[...]
        keep = jnp.where(row >= half, kr[1:2, :], kr[0:1, :])
        own = cm_ref[0]
        nxt_m = cm_ref[1]
        prv_m = cm_ref[2]

        def relax(values, rec, mat, keep_factor):
            rebuilt = jnp.dot(rec, mat, preferred_element_type=jnp.float32)
            return (keep_factor * values.astype(jnp.float32) + rebuilt).astype(jnp.bfloat16)

        def halo(nxt, prv, rec):
            up = jnp.dot(rec, nxt_m, preferred_element_type=jnp.float32)[half:]
            down = jnp.dot(rec, prv_m, preferred_element_type=jnp.float32)[:half]
            up = (kr[2:3, :] * nxt.astype(jnp.float32) + up).astype(jnp.bfloat16)
            down = (kr[3:4, :] * prv.astype(jnp.float32) + down).astype(jnp.bfloat16)
            return jnp.concatenate([down.astype(jnp.float32), up.astype(jnp.float32)], axis=0)

        rec_a_v = rec_a[0]
        rec_b_v = rec_b[0]
        relaxed_a = relax(cot_a[0], rec_a_v, own, keep)
        relaxed_b = relax(cot_b[0], rec_b_v, own, keep)
        edges = jnp.where(lane == 0, relaxed_b, relaxed_a)
        flipped = jnp.dot(flip_ref[...], edges, preferred_element_type=jnp.float32)
        edges32 = edges.astype(jnp.float32)
        source_a = jnp.where(face_ref[0] == 1, flipped, edges32)
        source_b = jnp.where(face_ref[1] == 1, flipped, edges32)
        ra = relaxed_a.astype(jnp.float32)
        rb = relaxed_b.astype(jnp.float32)
        near_a = jnp.where(lane == 0, source_a, pltpu.roll(ra, 1, 1))
        near_b = jnp.where(lane == cell_count - 1, source_b, pltpu.roll(rb, cell_count - 1, 1))
        base = col_ref[0]
        side = col_ref[1]
        zw_a = zw_ref[j]
        zw_b = zw_ref[node_count - 1 - j]
        halo_a = halo(nxt_a[0], prv_a[0], rec_a_v)
        halo_b = halo(nxt_b[0], prv_b[0], rec_b_v)
        res_a = (base - zw_a) * ra + side * halo_a
        res_a = res_a + zw_a * near_a
        res_b = (base - zw_b) * rb + side * halo_b
        res_b = res_b + zw_b * near_b
        slots[slot, 0] = res_a.astype(jnp.bfloat16)
        slots[slot, 1] = res_b.astype(jnp.bfloat16)
        for copy in copies(j, slot):
            copy.start()

        @pl.when(j == steps - 1)
        def _():
            if steps >= 2:
                for copy in copies(j - 1, 1 - slot):
                    copy.wait()
            for copy in copies(j, slot):
                copy.wait()

    lower = lambda j: (j, 0, 0)
    upper = lambda j: (node_count - 1 - j, 0, 0)
    fixed3 = lambda j: (0, 0, 0)
    fixed2 = lambda j: (0, 0)
    slab = (1, pair_count, cell_count)
    halo_slab = (1, half, cell_count)
    smem = pl.BlockSpec(memory_space=pltpu.SMEM)
    in_specs = [
        smem,
        smem,
        pl.BlockSpec(slab, lower),
        pl.BlockSpec(slab, upper),
        pl.BlockSpec(halo_slab, lower),
        pl.BlockSpec(halo_slab, upper),
        pl.BlockSpec(halo_slab, lower),
        pl.BlockSpec(halo_slab, upper),
        pl.BlockSpec(slab, lower),
        pl.BlockSpec(slab, upper),
        pl.BlockSpec(cross_mats.shape, fixed3),
        pl.BlockSpec(keep_rows.shape, fixed2),
        pl.BlockSpec(columns.shape, fixed3),
        pl.BlockSpec(flip.shape, fixed2),
    ]
    return pl.pallas_call(
        kernel,
        grid=(steps,),
        in_specs=in_specs,
        out_specs=pl.BlockSpec(memory_space=pl.ANY),
        out_shape=jax.ShapeDtypeStruct((node_count, pair_count, cell_count), jnp.bfloat16),
        scratch_shapes=[
            pltpu.VMEM((2, 2, pair_count, cell_count), jnp.bfloat16),
            pltpu.SemaphoreType.DMA((2, 2)),
        ],
        compiler_params=pltpu.CompilerParams(dimension_semantics=("arbitrary",)),
    )(z_weights, faces, field_in, field_in, got_next, got_next, got_prev, got_prev,
      recon_parts, recon_parts, cross_mats, keep_rows, columns, flip)


def solution(mesh):
    in_specs = (
        P("species", None, None, "space"),
        P("species"),
        P("species"),
        P(),
        P("space"),
        P("space"),
        P(None, "space"),
    )
    out_specs = P("species", None, None, "space")
    return jax.shard_map(
        on_device, mesh=mesh, in_specs=in_specs, out_specs=out_specs, check_vma=False
    )
```

```python
import math

import numpy as np
import jax
import jax.numpy as jnp
from jax import lax
from jax.experimental import pallas as pl
from jax.experimental.pallas import tpu as pltpu
from jax.sharding import PartitionSpec as P


NZ = 128

courant_max = 0.45
node_reach = 2.85


def passed_along(value, axis, steps):
    count = lax.axis_size(axis)
    pairs = [(source, (source + steps) % count) for source in range(count)]
    return lax.ppermute(value, axis, pairs)


def velocity_tables(node_count):
    pair_count = node_count * node_count
    spacing = 2.0 * node_reach / (node_count - 1)
    node_line = (np.arange(node_count, dtype=np.float64) - 0.5 * (node_count - 1)) * spacing
    grid_shape = (pair_count, node_count)
    along_x = np.broadcast_to(np.repeat(node_line, node_count)[:, None], grid_shape)
    along_y = np.broadcast_to(np.tile(node_line, node_count)[:, None], grid_shape)
    along_z = np.broadcast_to(node_line[None, :], grid_shape)
    square = along_x * along_x + along_y * along_y + along_z * along_z
    heat_term = square - 2.5
    functions = [
        np.ones(grid_shape),
        along_x,
        along_y,
        along_z,
        square - 1.5,
        along_x * along_y,
        along_x * along_z,
        along_y * along_z,
        along_x * along_x - along_y * along_y,
        along_y * along_y - along_z * along_z,
        along_x * heat_term,
        along_y * heat_term,
        along_z * heat_term,
    ]
    stacked = np.stack(functions)
    basis = stacked / np.sqrt(np.mean(stacked * stacked, axis=(1, 2), keepdims=True))
    weights = np.exp(-square) * (spacing * spacing * spacing) / math.pi**1.5
    recon = basis * weights[None]
    return node_line, basis, recon


def bf16_split(table, parts):
    rest = np.asarray(table, np.float64)
    pieces = []
    for _ in range(parts):
        piece = rest.astype(np.float32).astype(jnp.bfloat16).astype(np.float64)
        pieces.append(piece)
        rest = rest - piece
    return pieces


def on_device(cotangent, freq, ratio, coupling, wall, inlet, face_type):
    pair_count = cotangent.shape[1]
    node_count = cotangent.shape[2]
    cell_count = cotangent.shape[3]
    assert cell_count == NZ
    half = pair_count // 2
    moment_count = coupling.shape[2]
    species_count = lax.axis_size("species")

    node_line, basis, recon = velocity_tables(node_count)
    basis_k = np.transpose(basis, (0, 2, 1)).reshape(moment_count, node_count * pair_count)
    basis_parts = np.concatenate(bf16_split(basis_k, 3), axis=0)
    basis_parts = jnp.asarray(basis_parts.astype(jnp.bfloat16))
    weight_k = (recon[0] / basis[0]).T.reshape(-1).astype(np.float32)

    field_in = jnp.transpose(cotangent[0], (1, 0, 2))
    upper_in = field_in[:, half:, :]
    lower_in = field_in[:, :half, :]
    got_next = passed_along(upper_in, "space", -1)
    got_prev = passed_along(lower_in, "space", 1)

    open_cells = (1 - wall).astype(jnp.float32)
    keep_upper = open_cells * (1.0 - inlet.astype(jnp.float32))
    upward = (jnp.arange(pair_count) >= half)[None, :, None]
    keep = jnp.where(upward, keep_upper[None, None, :], open_cells[None, None, :])
    masked = field_in * keep.astype(jnp.bfloat16)
    parts = jnp.dot(
        basis_parts,
        masked.reshape(node_count * pair_count, cell_count),
        preferred_element_type=jnp.float32,
    )
    moments = parts[:moment_count] + parts[moment_count : 2 * moment_count] + parts[2 * moment_count :]

    species_index = lax.axis_index("species")
    row_k = lax.dynamic_index_in_dim(coupling, species_index, axis=0, keepdims=False)
    own_weight = lax.dynamic_index_in_dim(row_k, species_index, axis=0, keepdims=False)
    cross = own_weight[:, None] * moments
    for shift in range(1, species_count):
        source = (species_index - shift) % species_count
        other = passed_along(moments, "species", shift)
        weight = lax.dynamic_index_in_dim(row_k, source, axis=0, keepdims=False)
        cross = cross + weight[:, None] * other

    rows = 16
    assert moment_count + 2 < rows
    packet = jnp.concatenate(
        [
            cross,
            open_cells[None],
            keep_upper[None],
            jnp.zeros((rows - moment_count - 2, cell_count), jnp.float32),
        ],
        axis=0,
    )
    packet_next = passed_along(packet, "space", -1)
    packet_prev = passed_along(packet, "space", 1)

    rate_value = freq[0]
    scale_factor = courant_max * ratio[0] / node_reach
    line = jnp.asarray(node_line.astype(np.float32))
    pair_line = jnp.repeat(line, node_count)
    adv_x = jnp.abs(scale_factor * pair_line)
    adv_z = jnp.abs(scale_factor * line)
    columns = jnp.broadcast_to(
        jnp.stack([1.0 - adv_x, adv_x])[:, :, None], (2, pair_count, cell_count)
    )
    scalars = jnp.concatenate(
        [adv_z, jnp.zeros((31 - node_count,), jnp.float32), (1.0 - rate_value)[None]]
    )
    faces = face_type[:, 0]

    basis_run = lax.optimization_barrier(basis_parts).astype(jnp.float32)
    basis_sum = (
        basis_run[:moment_count] + basis_run[moment_count : 2 * moment_count]
    ) + basis_run[2 * moment_count :]
    recon_all = basis_sum * jnp.asarray(weight_k)[None]
    r1 = recon_all.astype(jnp.bfloat16)
    rest = recon_all - r1.astype(jnp.float32)
    r2 = rest.astype(jnp.bfloat16)
    r3 = (rest - r2.astype(jnp.float32)).astype(jnp.bfloat16)
    lanes = 128
    order = [0, 0, 1, 0, 1, 2]
    place = np.zeros((3 * moment_count, lanes), np.float32)
    for block, part in enumerate(order):
        for m in range(moment_count):
            place[part * moment_count + m, block * rows + m] = 1.0
    stacked_parts = jnp.concatenate([r1, r2, r3], axis=0)
    recon_parts = lax.dot_general(
        stacked_parts,
        jnp.asarray(place, jnp.bfloat16),
        (((0,), (0,)), ((), ())),
        preferred_element_type=jnp.float32,
    ).astype(jnp.bfloat16).reshape(node_count, pair_count, lanes)

    flip_rows = lax.broadcasted_iota(jnp.int32, (pair_count, pair_count), 0)
    flip_cols = lax.broadcasted_iota(jnp.int32, (pair_count, pair_count), 1)
    flip = (flip_rows + flip_cols == pair_count - 1).astype(jnp.bfloat16)

    partial = own_kernel(field_in, recon_parts, packet, columns, flip, scalars, faces)
    out = halo_kernel(partial, got_next, got_prev, recon_parts, packet_next, packet_prev, columns, scalars)
    return jnp.transpose(out, (1, 0, 2))[None]


def cross_matrix(packet, moment_count):
    rows = packet.shape[0]
    row = lax.broadcasted_iota(jnp.int32, packet.shape, 0)
    values = jnp.where(row < moment_count, packet, 0.0)
    c1 = values.astype(jnp.bfloat16)
    left = values - c1.astype(jnp.float32)
    c2 = left.astype(jnp.bfloat16)
    c3 = (left - c2.astype(jnp.float32)).astype(jnp.bfloat16)
    pad = jnp.zeros((128 - 6 * rows, packet.shape[1]), jnp.bfloat16)
    return jnp.concatenate([c1, c2, c1, c3, c2, c1, pad], axis=0)


def own_kernel(field_in, recon_parts, packet, columns, flip, scalars, faces):
    node_count, pair_count, cell_count = field_in.shape
    half = pair_count // 2
    steps = node_count // 2
    moment_count = packet.shape[0] - 3

    def kernel(sc_ref, face_ref, cot_a, cot_b, rec_a, rec_b, pk_ref, col_ref, flip_ref, out_ref):
        j = pl.program_id(0)
        row = lax.broadcasted_iota(jnp.int32, (pair_count, cell_count), 0)
        lane = lax.broadcasted_iota(jnp.int32, (pair_count, cell_count), 1)
        pk = pk_ref[...]
        rate = sc_ref[31]
        keep = rate * jnp.where(row >= half, pk[moment_count + 1 : moment_count + 2, :], pk[moment_count : moment_count + 1, :])
        own = cross_matrix(pk, moment_count)

        def relax(values, rec):
            rebuilt = jnp.dot(rec, own, preferred_element_type=jnp.float32)
            return (keep * values.astype(jnp.float32) + rebuilt).astype(jnp.bfloat16)

        relaxed_a = relax(cot_a[0], rec_a[0])
        relaxed_b = relax(cot_b[0], rec_b[0])
        edges = jnp.where(lane == 0, relaxed_b, relaxed_a)
        flipped = jnp.dot(flip_ref[...], edges, preferred_element_type=jnp.float32)
        edges32 = edges.astype(jnp.float32)
        source_a = jnp.where(face_ref[0] == 1, flipped, edges32)
        source_b = jnp.where(face_ref[1] == 1, flipped, edges32)
        ra = relaxed_a.astype(jnp.float32)
        rb = relaxed_b.astype(jnp.float32)
        near_a = jnp.where(lane == 0, source_a, pltpu.roll(ra, 1, 1))
        near_b = jnp.where(lane == cell_count - 1, source_b, pltpu.roll(rb, cell_count - 1, 1))
        base = col_ref[0]
        zw_a = sc_ref[j]
        zw_b = sc_ref[node_count - 1 - j]
        out_ref[0, 0] = (base - zw_a) * ra + zw_a * near_a
        out_ref[0, 1] = (base - zw_b) * rb + zw_b * near_b

    lower = lambda j: (j, 0, 0)
    upper = lambda j: (node_count - 1 - j, 0, 0)
    slab = (1, pair_count, cell_count)
    smem = pl.BlockSpec(memory_space=pltpu.SMEM)
    in_specs = [
        smem,
        smem,
        pl.BlockSpec(slab, lower),
        pl.BlockSpec(slab, upper),
        pl.BlockSpec(slab, lower),
        pl.BlockSpec(slab, upper),
        pl.BlockSpec(packet.shape, lambda j: (0, 0)),
        pl.BlockSpec(slab, lambda j: (0, 0, 0)),
        pl.BlockSpec(flip.shape, lambda j: (0, 0)),
    ]
    return pl.pallas_call(
        kernel,
        grid=(steps,),
        in_specs=in_specs,
        out_specs=pl.BlockSpec((1, 2, pair_count, cell_count), lambda j: (j, 0, 0, 0)),
        out_shape=jax.ShapeDtypeStruct((steps, 2, pair_count, cell_count), jnp.float32),
        compiler_params=pltpu.CompilerParams(dimension_semantics=("arbitrary",)),
    )(scalars, faces, field_in, field_in, recon_parts, recon_parts, packet, columns, flip)


def halo_kernel(partial, got_next, got_prev, recon_parts, packet_next, packet_prev, columns, scalars):
    node_count, half, cell_count = got_next.shape
    pair_count = 2 * half
    steps = node_count // 2
    moment_count = packet_next.shape[0] - 3

    def kernel(sc_ref, part_ref, nxt_ref, prv_ref, rec_ref, pn_ref, pp_ref, col_ref, out_ref):
        rate = sc_ref[31]
        pn = pn_ref[...]
        pp = pp_ref[...]
        rec = rec_ref[0]
        up = jnp.dot(rec, cross_matrix(pn, moment_count), preferred_element_type=jnp.float32)[half:]
        down = jnp.dot(rec, cross_matrix(pp, moment_count), preferred_element_type=jnp.float32)[:half]
        keep_up = rate * pn[moment_count + 1 : moment_count + 2, :]
        keep_down = rate * pp[moment_count : moment_count + 1, :]
        up = (keep_up * nxt_ref[0].astype(jnp.float32) + up).astype(jnp.bfloat16)
        down = (keep_down * prv_ref[0].astype(jnp.float32) + down).astype(jnp.bfloat16)
        shifted = jnp.concatenate([down.astype(jnp.float32), up.astype(jnp.float32)], axis=0)
        out_ref[0] = (part_ref[0, 0] + col_ref[0] * shifted).astype(jnp.bfloat16)

    def pair_of(i):
        return (jnp.where(i < steps, i, node_count - 1 - i), jnp.where(i < steps, 0, 1), 0, 0)

    smem = pl.BlockSpec(memory_space=pltpu.SMEM)
    in_specs = [
        smem,
        pl.BlockSpec((1, 1, pair_count, cell_count), pair_of),
        pl.BlockSpec((1, half, cell_count), lambda i: (i, 0, 0)),
        pl.BlockSpec((1, half, cell_count), lambda i: (i, 0, 0)),
        pl.BlockSpec((1, pair_count, cell_count), lambda i: (i, 0, 0)),
        pl.BlockSpec(packet_next.shape, lambda i: (0, 0)),
        pl.BlockSpec(packet_prev.shape, lambda i: (0, 0)),
        pl.BlockSpec((1, pair_count, cell_count), lambda i: (1, 0, 0)),
    ]
    return pl.pallas_call(
        kernel,
        grid=(node_count,),
        in_specs=in_specs,
        out_specs=pl.BlockSpec((1, pair_count, cell_count), lambda i: (i, 0, 0)),
        out_shape=jax.ShapeDtypeStruct((node_count, pair_count, cell_count), jnp.bfloat16),
        compiler_params=pltpu.CompilerParams(dimension_semantics=("arbitrary",)),
    )(scalars, partial, got_next, got_prev, recon_parts, packet_next, packet_prev, columns)


def solution(mesh):
    in_specs = (
        P("species", None, None, "space"),
        P("species"),
        P("species"),
        P(),
        P("space"),
        P("space"),
        P(None, "space"),
    )
    out_specs = P("species", None, None, "space")

    return jax.shard_map(on_device, mesh=mesh, in_specs=in_specs, out_specs=out_specs, check_vma=False)
```

```python
import math

import numpy as np
import jax
import jax.numpy as jnp
from jax import lax
from jax.experimental import pallas as pl
from jax.experimental.pallas import tpu as pltpu
from jax.sharding import PartitionSpec as P


NZ = 128

courant_max = 0.45
node_reach = 2.85


def passed_along(value, axis, steps):
    count = lax.axis_size(axis)
    pairs = [(source, (source + steps) % count) for source in range(count)]
    return lax.ppermute(value, axis, pairs)


def velocity_tables(node_count):
    pair_count = node_count * node_count
    spacing = 2.0 * node_reach / (node_count - 1)
    node_line = (np.arange(node_count, dtype=np.float64) - 0.5 * (node_count - 1)) * spacing
    grid_shape = (pair_count, node_count)
    along_x = np.broadcast_to(np.repeat(node_line, node_count)[:, None], grid_shape)
    along_y = np.broadcast_to(np.tile(node_line, node_count)[:, None], grid_shape)
    along_z = np.broadcast_to(node_line[None, :], grid_shape)
    square = along_x * along_x + along_y * along_y + along_z * along_z
    heat_term = square - 2.5
    functions = [
        np.ones(grid_shape),
        along_x,
        along_y,
        along_z,
        square - 1.5,
        along_x * along_y,
        along_x * along_z,
        along_y * along_z,
        along_x * along_x - along_y * along_y,
        along_y * along_y - along_z * along_z,
        along_x * heat_term,
        along_y * heat_term,
        along_z * heat_term,
    ]
    stacked = np.stack(functions)
    basis = stacked / np.sqrt(np.mean(stacked * stacked, axis=(1, 2), keepdims=True))
    weights = np.exp(-square) * (spacing * spacing * spacing) / math.pi**1.5
    recon = basis * weights[None]
    return node_line, basis, recon


def bf16_split(table, parts):
    rest = np.asarray(table, np.float64)
    pieces = []
    for _ in range(parts):
        piece = rest.astype(np.float32).astype(jnp.bfloat16).astype(np.float64)
        pieces.append(piece)
        rest = rest - piece
    return pieces


def on_device(cotangent, freq, ratio, coupling, wall, inlet, face_type):
    pair_count = cotangent.shape[1]
    node_count = cotangent.shape[2]
    cell_count = cotangent.shape[3]
    assert cell_count == NZ
    half = pair_count // 2
    moment_count = coupling.shape[2]
    species_count = lax.axis_size("species")

    node_line, basis, recon = velocity_tables(node_count)
    basis_k = np.transpose(basis, (0, 2, 1)).reshape(moment_count, node_count * pair_count)
    basis_parts = np.concatenate(bf16_split(basis_k, 3), axis=0)
    basis_parts = jnp.asarray(basis_parts.astype(jnp.bfloat16))
    weight_k = (recon[0] / basis[0]).T.reshape(-1).astype(np.float32)

    field_in = jnp.transpose(cotangent[0], (1, 0, 2))
    upper_in = field_in[:, half:, :]
    lower_in = field_in[:, :half, :]
    got_next = passed_along(upper_in, "space", -1)
    got_prev = passed_along(lower_in, "space", 1)

    open_cells = (1 - wall).astype(jnp.float32)
    keep_upper = open_cells * (1.0 - inlet.astype(jnp.float32))
    upward = (jnp.arange(pair_count) >= half)[None, :, None]
    keep = jnp.where(upward, keep_upper[None, None, :], open_cells[None, None, :])
    masked = field_in * keep.astype(jnp.bfloat16)
    parts = jnp.dot(
        basis_parts,
        masked.reshape(node_count * pair_count, cell_count),
        preferred_element_type=jnp.float32,
    )
    moments = parts[:moment_count] + parts[moment_count : 2 * moment_count] + parts[2 * moment_count :]

    species_index = lax.axis_index("species")
    row_k = lax.dynamic_index_in_dim(coupling, species_index, axis=0, keepdims=False)
    own_weight = lax.dynamic_index_in_dim(row_k, species_index, axis=0, keepdims=False)
    cross = own_weight[:, None] * moments
    for shift in range(1, species_count):
        source = (species_index - shift) % species_count
        other = passed_along(moments, "species", shift)
        weight = lax.dynamic_index_in_dim(row_k, source, axis=0, keepdims=False)
        cross = cross + weight[:, None] * other

    rows = 16
    assert moment_count + 2 < rows
    packet = jnp.concatenate(
        [
            cross,
            open_cells[None],
            keep_upper[None],
            jnp.zeros((rows - moment_count - 2, cell_count), jnp.float32),
        ],
        axis=0,
    )
    packet_next = passed_along(packet, "space", -1)
    packet_prev = passed_along(packet, "space", 1)

    rate_value = freq[0]
    scale_factor = courant_max * ratio[0] / node_reach
    line = jnp.asarray(node_line.astype(np.float32))
    pair_line = jnp.repeat(line, node_count)
    adv_x = jnp.abs(scale_factor * pair_line)
    adv_z = jnp.abs(scale_factor * line)
    columns = jnp.broadcast_to(
        jnp.stack([1.0 - adv_x, adv_x])[:, :, None], (2, pair_count, cell_count)
    )
    scalars = jnp.concatenate(
        [adv_z, jnp.zeros((31 - node_count,), jnp.float32), (1.0 - rate_value)[None]]
    )
    faces = face_type[:, 0]

    basis_run = lax.optimization_barrier(basis_parts).astype(jnp.float32)
    basis_sum = (
        basis_run[:moment_count] + basis_run[moment_count : 2 * moment_count]
    ) + basis_run[2 * moment_count :]
    recon_all = basis_sum * jnp.asarray(weight_k)[None]
    r1 = recon_all.astype(jnp.bfloat16)
    rest = recon_all - r1.astype(jnp.float32)
    r2 = rest.astype(jnp.bfloat16)
    r3 = (rest - r2.astype(jnp.float32)).astype(jnp.bfloat16)
    lanes = 128
    order = [0, 0, 1, 0, 1, 2]
    place = np.zeros((3 * moment_count, lanes), np.float32)
    for block, part in enumerate(order):
        for m in range(moment_count):
            place[part * moment_count + m, block * rows + m] = 1.0
    stacked_parts = jnp.concatenate([r1, r2, r3], axis=0)
    recon_parts = lax.dot_general(
        stacked_parts,
        jnp.asarray(place, jnp.bfloat16),
        (((0,), (0,)), ((), ())),
        preferred_element_type=jnp.float32,
    ).astype(jnp.bfloat16).reshape(node_count, pair_count, lanes)

    flip_rows = lax.broadcasted_iota(jnp.int32, (pair_count, pair_count), 0)
    flip_cols = lax.broadcasted_iota(jnp.int32, (pair_count, pair_count), 1)
    flip = (flip_rows + flip_cols == pair_count - 1).astype(jnp.bfloat16)

    recon_halves = recon_parts.reshape(node_count, 2, half, lanes)
    partial_lower, partial_upper = own_kernel(
        field_in, recon_parts, packet, columns, flip, scalars, faces
    )
    out = halo_kernel(
        partial_lower, partial_upper, got_next, got_prev, recon_halves, packet_next, packet_prev,
        columns, scalars,
    )
    return jnp.transpose(out, (1, 0, 2))[None]


def cross_matrix(packet, moment_count):
    rows = packet.shape[0]
    row = lax.broadcasted_iota(jnp.int32, packet.shape, 0)
    values = jnp.where(row < moment_count, packet, 0.0)
    c1 = values.astype(jnp.bfloat16)
    left = values - c1.astype(jnp.float32)
    c2 = left.astype(jnp.bfloat16)
    c3 = (left - c2.astype(jnp.float32)).astype(jnp.bfloat16)
    pad = jnp.zeros((128 - 6 * rows, packet.shape[1]), jnp.bfloat16)
    return jnp.concatenate([c1, c2, c1, c3, c2, c1, pad], axis=0)


def own_kernel(field_in, recon_parts, packet, columns, flip, scalars, faces):
    node_count, pair_count, cell_count = field_in.shape
    half = pair_count // 2
    steps = node_count // 2
    moment_count = packet.shape[0] - 3
    group = 5 if steps % 5 == 0 else 1
    blocks = steps // group

    def kernel(sc_ref, face_ref, cot_lo, cot_hi, rec_lo, rec_hi, pk_ref, col_ref, flip_ref, out_lo, out_hi):
        b = pl.program_id(0)
        row = lax.broadcasted_iota(jnp.int32, (pair_count, cell_count), 0)
        lane = lax.broadcasted_iota(jnp.int32, (pair_count, cell_count), 1)
        pk = pk_ref[...]
        rate = sc_ref[31]
        keep = rate * jnp.where(row >= half, pk[moment_count + 1 : moment_count + 2, :], pk[moment_count : moment_count + 1, :])
        own = cross_matrix(pk, moment_count)
        base = col_ref[0]
        face_a = face_ref[0] == 1
        face_b = face_ref[1] == 1

        def relax(values, rec):
            rebuilt = jnp.dot(rec, own, preferred_element_type=jnp.float32)
            return (keep * values.astype(jnp.float32) + rebuilt).astype(jnp.bfloat16)

        def one(t, carry):
            u = group - 1 - t
            j = b * group + t
            relaxed_a = relax(cot_lo[t], rec_lo[t])
            relaxed_b = relax(cot_hi[u], rec_hi[u])
            edges = jnp.where(lane == 0, relaxed_b, relaxed_a)
            flipped = jnp.dot(flip_ref[...], edges, preferred_element_type=jnp.float32)
            edges32 = edges.astype(jnp.float32)
            source_a = jnp.where(face_a, flipped, edges32)
            source_b = jnp.where(face_b, flipped, edges32)
            ra = relaxed_a.astype(jnp.float32)
            rb = relaxed_b.astype(jnp.float32)
            near_a = jnp.where(lane == 0, source_a, pltpu.roll(ra, 1, 1))
            near_b = jnp.where(lane == cell_count - 1, source_b, pltpu.roll(rb, cell_count - 1, 1))
            zw_a = sc_ref[j]
            zw_b = sc_ref[node_count - 1 - j]
            out_lo[t] = (base - zw_a) * ra + zw_a * near_a
            out_hi[u] = (base - zw_b) * rb + zw_b * near_b
            return carry

        lax.fori_loop(0, group, one, 0)

    block = (group, pair_count, cell_count)
    smem = pl.BlockSpec(memory_space=pltpu.SMEM)
    in_specs = [
        smem,
        smem,
        pl.BlockSpec(block, lambda b: (b, 0, 0)),
        pl.BlockSpec(block, lambda b: (2 * blocks - 1 - b, 0, 0)),
        pl.BlockSpec(block, lambda b: (b, 0, 0)),
        pl.BlockSpec(block, lambda b: (2 * blocks - 1 - b, 0, 0)),
        pl.BlockSpec(packet.shape, lambda b: (0, 0)),
        pl.BlockSpec((1, pair_count, cell_count), lambda b: (0, 0, 0)),
        pl.BlockSpec(flip.shape, lambda b: (0, 0)),
    ]
    out_specs = [
        pl.BlockSpec(block, lambda b: (b, 0, 0)),
        pl.BlockSpec(block, lambda b: (blocks - 1 - b, 0, 0)),
    ]
    shape = jax.ShapeDtypeStruct((steps, pair_count, cell_count), jnp.float32)
    return pl.pallas_call(
        kernel,
        grid=(blocks,),
        in_specs=in_specs,
        out_specs=out_specs,
        out_shape=[shape, shape],
        compiler_params=pltpu.CompilerParams(
            dimension_semantics=("arbitrary",), vmem_limit_bytes=48 * 1024 * 1024
        ),
    )(scalars, faces, field_in, field_in, recon_parts, recon_parts, packet, columns, flip)


def halo_kernel(partial_lower, partial_upper, got_next, got_prev, recon_halves, packet_next, packet_prev, columns, scalars):
    node_count, half, cell_count = got_next.shape
    pair_count = 2 * half
    steps = node_count // 2
    moment_count = packet_next.shape[0] - 3
    group = 5 if steps % 5 == 0 else 1
    blocks = node_count // group
    lower_blocks = steps // group

    def kernel(sc_ref, plo_ref, phi_ref, nxt_ref, prv_ref, rec_ref, pn_ref, pp_ref, col_ref, out_ref):
        i = pl.program_id(0)
        rate = sc_ref[31]
        pn = pn_ref[...]
        pp = pp_ref[...]
        next_mat = cross_matrix(pn, moment_count)
        prev_mat = cross_matrix(pp, moment_count)
        keep_up = rate * pn[moment_count + 1 : moment_count + 2, :]
        keep_down = rate * pp[moment_count : moment_count + 1, :]
        side = col_ref[0]

        def run(part_ref):
            def one(t, carry):
                up = jnp.dot(rec_ref[t, 1], next_mat, preferred_element_type=jnp.float32)
                down = jnp.dot(rec_ref[t, 0], prev_mat, preferred_element_type=jnp.float32)
                up = (keep_up * nxt_ref[t].astype(jnp.float32) + up).astype(jnp.bfloat16)
                down = (keep_down * prv_ref[t].astype(jnp.float32) + down).astype(jnp.bfloat16)
                shifted = jnp.concatenate([down.astype(jnp.float32), up.astype(jnp.float32)], axis=0)
                out_ref[t] = (part_ref[t] + side * shifted).astype(jnp.bfloat16)
                return carry

            lax.fori_loop(0, group, one, 0)

        @pl.when(i < lower_blocks)
        def _():
            run(plo_ref)

        @pl.when(i >= lower_blocks)
        def _():
            run(phi_ref)

    block = (group, pair_count, cell_count)
    smem = pl.BlockSpec(memory_space=pltpu.SMEM)
    in_specs = [
        smem,
        pl.BlockSpec(block, lambda i: (jnp.minimum(i, lower_blocks - 1), 0, 0)),
        pl.BlockSpec(block, lambda i: (jnp.maximum(i - lower_blocks, 0), 0, 0)),
        pl.BlockSpec((group, half, cell_count), lambda i: (i, 0, 0)),
        pl.BlockSpec((group, half, cell_count), lambda i: (i, 0, 0)),
        pl.BlockSpec((group, 2, half, recon_halves.shape[3]), lambda i: (i, 0, 0, 0)),
        pl.BlockSpec(packet_next.shape, lambda i: (0, 0)),
        pl.BlockSpec(packet_prev.shape, lambda i: (0, 0)),
        pl.BlockSpec((1, pair_count, cell_count), lambda i: (1, 0, 0)),
    ]
    return pl.pallas_call(
        kernel,
        grid=(blocks,),
        in_specs=in_specs,
        out_specs=pl.BlockSpec(block, lambda i: (i, 0, 0)),
        out_shape=jax.ShapeDtypeStruct((node_count, pair_count, cell_count), jnp.bfloat16),
        compiler_params=pltpu.CompilerParams(
            dimension_semantics=("arbitrary",), vmem_limit_bytes=48 * 1024 * 1024
        ),
    )(scalars, partial_lower, partial_upper, got_next, got_prev, recon_halves, packet_next, packet_prev, columns)


def solution(mesh):
    in_specs = (
        P("species", None, None, "space"),
        P("species"),
        P("species"),
        P(),
        P("space"),
        P("space"),
        P(None, "space"),
    )
    out_specs = P("species", None, None, "space")

    return jax.shard_map(on_device, mesh=mesh, in_specs=in_specs, out_specs=out_specs, check_vma=False)
```

```python
import math

import numpy as np
import jax
import jax.numpy as jnp
from jax import lax
from jax.experimental import pallas as pl
from jax.experimental.pallas import tpu as pltpu
from jax.sharding import PartitionSpec as P


NZ = 128

courant_max = 0.45
node_reach = 2.85


def passed_along(value, axis, steps):
    count = lax.axis_size(axis)
    pairs = [(source, (source + steps) % count) for source in range(count)]
    return lax.ppermute(value, axis, pairs)


def velocity_tables(node_count):
    pair_count = node_count * node_count
    spacing = 2.0 * node_reach / (node_count - 1)
    node_line = (np.arange(node_count, dtype=np.float64) - 0.5 * (node_count - 1)) * spacing
    grid_shape = (pair_count, node_count)
    along_x = np.broadcast_to(np.repeat(node_line, node_count)[:, None], grid_shape)
    along_y = np.broadcast_to(np.tile(node_line, node_count)[:, None], grid_shape)
    along_z = np.broadcast_to(node_line[None, :], grid_shape)
    square = along_x * along_x + along_y * along_y + along_z * along_z
    heat_term = square - 2.5
    functions = [
        np.ones(grid_shape),
        along_x,
        along_y,
        along_z,
        square - 1.5,
        along_x * along_y,
        along_x * along_z,
        along_y * along_z,
        along_x * along_x - along_y * along_y,
        along_y * along_y - along_z * along_z,
        along_x * heat_term,
        along_y * heat_term,
        along_z * heat_term,
    ]
    stacked = np.stack(functions)
    basis = stacked / np.sqrt(np.mean(stacked * stacked, axis=(1, 2), keepdims=True))
    weights = np.exp(-square) * (spacing * spacing * spacing) / math.pi**1.5
    recon = basis * weights[None]
    return node_line, basis, recon


def bf16_split(table, parts):
    rest = np.asarray(table, np.float64)
    pieces = []
    for _ in range(parts):
        piece = rest.astype(np.float32).astype(jnp.bfloat16).astype(np.float64)
        pieces.append(piece)
        rest = rest - piece
    return pieces


def on_device(cotangent, freq, ratio, coupling, wall, inlet, face_type):
    pair_count = cotangent.shape[1]
    node_count = cotangent.shape[2]
    cell_count = cotangent.shape[3]
    assert cell_count == NZ
    half = pair_count // 2
    moment_count = coupling.shape[2]
    species_count = lax.axis_size("species")

    node_line, basis, recon = velocity_tables(node_count)
    basis_k = np.transpose(basis, (0, 2, 1)).reshape(moment_count, node_count * pair_count)
    basis_parts = np.concatenate(bf16_split(basis_k, 3), axis=0)
    basis_parts = jnp.asarray(basis_parts.astype(jnp.bfloat16))
    weight_k = (recon[0] / basis[0]).T.reshape(-1).astype(np.float32)

    field_in = jnp.transpose(cotangent[0], (1, 0, 2))
    upper_in = field_in[:, half:, :]
    lower_in = field_in[:, :half, :]
    got_next = passed_along(upper_in, "space", -1)
    got_prev = passed_along(lower_in, "space", 1)

    open_cells = (1 - wall).astype(jnp.float32)
    keep_upper = open_cells * (1.0 - inlet.astype(jnp.float32))
    upward = (jnp.arange(pair_count) >= half)[None, :, None]
    keep = jnp.where(upward, keep_upper[None, None, :], open_cells[None, None, :])
    masked = field_in * keep.astype(jnp.bfloat16)
    parts = jnp.dot(
        basis_parts,
        masked.reshape(node_count * pair_count, cell_count),
        preferred_element_type=jnp.float32,
    )
    moments = parts[:moment_count] + parts[moment_count : 2 * moment_count] + parts[2 * moment_count :]

    species_index = lax.axis_index("species")
    row_k = lax.dynamic_index_in_dim(coupling, species_index, axis=0, keepdims=False)
    everyone = lax.all_to_all(
        jnp.broadcast_to(moments[None], (species_count,) + moments.shape),
        "species",
        0,
        0,
        tiled=True,
    )
    cross = jnp.sum(row_k[:, :, None] * everyone, axis=0)

    rows = 16
    assert moment_count + 2 < rows
    packet = jnp.concatenate(
        [
            cross,
            open_cells[None],
            keep_upper[None],
            jnp.zeros((rows - moment_count - 2, cell_count), jnp.float32),
        ],
        axis=0,
    )
    packet_next = passed_along(packet, "space", -1)
    packet_prev = passed_along(packet, "space", 1)

    rate_value = freq[0]
    scale_factor = courant_max * ratio[0] / node_reach
    line = jnp.asarray(node_line.astype(np.float32))
    pair_line = jnp.repeat(line, node_count)
    adv_x = jnp.abs(scale_factor * pair_line)
    adv_z = jnp.abs(scale_factor * line)
    columns = jnp.broadcast_to(
        jnp.stack([1.0 - adv_x, adv_x])[:, :, None], (2, pair_count, cell_count)
    )
    scalars = jnp.concatenate(
        [adv_z, jnp.zeros((31 - node_count,), jnp.float32), (1.0 - rate_value)[None]]
    )
    faces = face_type[:, 0]

    lanes = 128
    recon_halves = jnp.asarray(packed_recon(recon, rows, lanes))

    flip_rows = lax.broadcasted_iota(jnp.int32, (pair_count, pair_count), 0)
    flip_cols = lax.broadcasted_iota(jnp.int32, (pair_count, pair_count), 1)
    flip = (flip_rows + flip_cols == pair_count - 1).astype(jnp.bfloat16)

    partial_lower, partial_upper = own_kernel(
        field_in, recon_halves, packet, columns, flip, scalars, faces
    )
    out = halo_kernel(
        partial_lower, partial_upper, got_next, got_prev, recon_halves, packet_next, packet_prev,
        columns, scalars,
    )
    return jnp.transpose(out, (1, 0, 2))[None]


def packed_recon(recon, rows, lanes):
    moment_count, pair_count, node_count = recon.shape
    half = pair_count // 2
    table = np.transpose(recon, (2, 1, 0))
    parts = bf16_split(table, 3)
    order = [0, 0, 1, 0, 1, 2]
    packed = np.zeros((node_count, pair_count, lanes), np.float32)
    for block, part in enumerate(order):
        packed[:, :, block * rows : block * rows + moment_count] = parts[part]
    packed = packed.reshape(node_count, 2, half, lanes)
    return packed.astype(jnp.bfloat16)


def cross_matrix(packet, moment_count):
    rows = packet.shape[0]
    row = lax.broadcasted_iota(jnp.int32, packet.shape, 0)
    values = jnp.where(row < moment_count, packet, 0.0)
    c1 = values.astype(jnp.bfloat16)
    left = values - c1.astype(jnp.float32)
    c2 = left.astype(jnp.bfloat16)
    c3 = (left - c2.astype(jnp.float32)).astype(jnp.bfloat16)
    pad = jnp.zeros((128 - 6 * rows, packet.shape[1]), jnp.bfloat16)
    return jnp.concatenate([c1, c2, c1, c3, c2, c1, pad], axis=0)


def own_kernel(field_in, recon_halves, packet, columns, flip, scalars, faces):
    node_count, pair_count, cell_count = field_in.shape
    half = pair_count // 2
    steps = node_count // 2
    moment_count = packet.shape[0] - 3
    group = 5 if steps % 5 == 0 else 1
    blocks = steps // group

    def kernel(sc_ref, face_ref, cot_lo, cot_hi, rec_lo, rec_hi, pk_ref, col_ref, flip_ref, out_lo, out_hi):
        b = pl.program_id(0)
        row = lax.broadcasted_iota(jnp.int32, (pair_count, cell_count), 0)
        lane = lax.broadcasted_iota(jnp.int32, (pair_count, cell_count), 1)
        pk = pk_ref[...]
        rate = sc_ref[31]
        keep = rate * jnp.where(row >= half, pk[moment_count + 1 : moment_count + 2, :], pk[moment_count : moment_count + 1, :])
        own = cross_matrix(pk, moment_count)
        base = col_ref[0]
        face_a = face_ref[0] == 1
        face_b = face_ref[1] == 1

        def relax(values, rec_ref, at):
            rebuilt = jnp.concatenate(
                [
                    jnp.dot(rec_ref[at, 0], own, preferred_element_type=jnp.float32),
                    jnp.dot(rec_ref[at, 1], own, preferred_element_type=jnp.float32),
                ],
                axis=0,
            )
            return (keep * values.astype(jnp.float32) + rebuilt).astype(jnp.bfloat16)

        def one(t, carry):
            u = group - 1 - t
            j = b * group + t
            relaxed_a = relax(cot_lo[t], rec_lo, t)
            relaxed_b = relax(cot_hi[u], rec_hi, u)
            edges = jnp.where(lane == 0, relaxed_b, relaxed_a)
            flipped = jnp.dot(flip_ref[...], edges, preferred_element_type=jnp.float32)
            edges32 = edges.astype(jnp.float32)
            source_a = jnp.where(face_a, flipped, edges32)
            source_b = jnp.where(face_b, flipped, edges32)
            ra = relaxed_a.astype(jnp.float32)
            rb = relaxed_b.astype(jnp.float32)
            near_a = jnp.where(lane == 0, source_a, pltpu.roll(ra, 1, 1))
            near_b = jnp.where(lane == cell_count - 1, source_b, pltpu.roll(rb, cell_count - 1, 1))
            zw_a = sc_ref[j]
            zw_b = sc_ref[node_count - 1 - j]
            out_lo[t] = (base - zw_a) * ra + zw_a * near_a
            out_hi[u] = (base - zw_b) * rb + zw_b * near_b
            return carry

        lax.fori_loop(0, group, one, 0)

    block = (group, pair_count, cell_count)
    smem = pl.BlockSpec(memory_space=pltpu.SMEM)
    in_specs = [
        smem,
        smem,
        pl.BlockSpec(block, lambda b: (b, 0, 0)),
        pl.BlockSpec(block, lambda b: (2 * blocks - 1 - b, 0, 0)),
        pl.BlockSpec((group, 2, half, recon_halves.shape[3]), lambda b: (b, 0, 0, 0)),
        pl.BlockSpec((group, 2, half, recon_halves.shape[3]), lambda b: (2 * blocks - 1 - b, 0, 0, 0)),
        pl.BlockSpec(packet.shape, lambda b: (0, 0)),
        pl.BlockSpec((1, pair_count, cell_count), lambda b: (0, 0, 0)),
        pl.BlockSpec(flip.shape, lambda b: (0, 0)),
    ]
    out_specs = [
        pl.BlockSpec(block, lambda b: (b, 0, 0)),
        pl.BlockSpec(block, lambda b: (blocks - 1 - b, 0, 0)),
    ]
    shape = jax.ShapeDtypeStruct((steps, pair_count, cell_count), jnp.float32)
    return pl.pallas_call(
        kernel,
        grid=(blocks,),
        in_specs=in_specs,
        out_specs=out_specs,
        out_shape=[shape, shape],
        compiler_params=pltpu.CompilerParams(
            dimension_semantics=("arbitrary",), vmem_limit_bytes=48 * 1024 * 1024
        ),
    )(scalars, faces, field_in, field_in, recon_halves, recon_halves, packet, columns, flip)


def halo_kernel(partial_lower, partial_upper, got_next, got_prev, recon_halves, packet_next, packet_prev, columns, scalars):
    node_count, half, cell_count = got_next.shape
    pair_count = 2 * half
    steps = node_count // 2
    moment_count = packet_next.shape[0] - 3
    group = 5 if steps % 5 == 0 else 1
    blocks = node_count // group
    lower_blocks = steps // group

    def kernel(sc_ref, plo_ref, phi_ref, nxt_ref, prv_ref, rec_ref, pn_ref, pp_ref, col_ref, out_ref):
        i = pl.program_id(0)
        rate = sc_ref[31]
        pn = pn_ref[...]
        pp = pp_ref[...]
        next_mat = cross_matrix(pn, moment_count)
        prev_mat = cross_matrix(pp, moment_count)
        keep_up = rate * pn[moment_count + 1 : moment_count + 2, :]
        keep_down = rate * pp[moment_count : moment_count + 1, :]
        side = col_ref[0]

        def run(part_ref):
            def one(t, carry):
                up = jnp.dot(rec_ref[t, 1], next_mat, preferred_element_type=jnp.float32)
                down = jnp.dot(rec_ref[t, 0], prev_mat, preferred_element_type=jnp.float32)
                up = (keep_up * nxt_ref[t].astype(jnp.float32) + up).astype(jnp.bfloat16)
                down = (keep_down * prv_ref[t].astype(jnp.float32) + down).astype(jnp.bfloat16)
                shifted = jnp.concatenate([down.astype(jnp.float32), up.astype(jnp.float32)], axis=0)
                out_ref[t] = (part_ref[t] + side * shifted).astype(jnp.bfloat16)
                return carry

            lax.fori_loop(0, group, one, 0)

        @pl.when(i < lower_blocks)
        def _():
            run(plo_ref)

        @pl.when(i >= lower_blocks)
        def _():
            run(phi_ref)

    block = (group, pair_count, cell_count)
    smem = pl.BlockSpec(memory_space=pltpu.SMEM)
    in_specs = [
        smem,
        pl.BlockSpec(block, lambda i: (jnp.minimum(i, lower_blocks - 1), 0, 0)),
        pl.BlockSpec(block, lambda i: (jnp.maximum(i - lower_blocks, 0), 0, 0)),
        pl.BlockSpec((group, half, cell_count), lambda i: (i, 0, 0)),
        pl.BlockSpec((group, half, cell_count), lambda i: (i, 0, 0)),
        pl.BlockSpec((group, 2, half, recon_halves.shape[3]), lambda i: (i, 0, 0, 0)),
        pl.BlockSpec(packet_next.shape, lambda i: (0, 0)),
        pl.BlockSpec(packet_prev.shape, lambda i: (0, 0)),
        pl.BlockSpec((1, pair_count, cell_count), lambda i: (1, 0, 0)),
    ]
    return pl.pallas_call(
        kernel,
        grid=(blocks,),
        in_specs=in_specs,
        out_specs=pl.BlockSpec(block, lambda i: (i, 0, 0)),
        out_shape=jax.ShapeDtypeStruct((node_count, pair_count, cell_count), jnp.bfloat16),
        compiler_params=pltpu.CompilerParams(
            dimension_semantics=("arbitrary",), vmem_limit_bytes=48 * 1024 * 1024
        ),
    )(scalars, partial_lower, partial_upper, got_next, got_prev, recon_halves, packet_next, packet_prev, columns)


def solution(mesh):
    in_specs = (
        P("species", None, None, "space"),
        P("species"),
        P("species"),
        P(),
        P("space"),
        P("space"),
        P(None, "space"),
    )
    out_specs = P("species", None, None, "space")

    return jax.shard_map(on_device, mesh=mesh, in_specs=in_specs, out_specs=out_specs, check_vma=False)
```

```python
import math

import numpy as np
import jax
import jax.numpy as jnp
from jax import lax
from jax.experimental import pallas as pl
from jax.experimental.pallas import tpu as pltpu
from jax.sharding import PartitionSpec as P


NZ = 128

courant_max = 0.45
node_reach = 2.85


def passed_along(value, axis, steps):
    count = lax.axis_size(axis)
    pairs = [(source, (source + steps) % count) for source in range(count)]
    return lax.ppermute(value, axis, pairs)


def velocity_tables(node_count):
    pair_count = node_count * node_count
    spacing = 2.0 * node_reach / (node_count - 1)
    node_line = (np.arange(node_count, dtype=np.float64) - 0.5 * (node_count - 1)) * spacing
    grid_shape = (pair_count, node_count)
    along_x = np.broadcast_to(np.repeat(node_line, node_count)[:, None], grid_shape)
    along_y = np.broadcast_to(np.tile(node_line, node_count)[:, None], grid_shape)
    along_z = np.broadcast_to(node_line[None, :], grid_shape)
    square = along_x * along_x + along_y * along_y + along_z * along_z
    heat_term = square - 2.5
    functions = [
        np.ones(grid_shape),
        along_x,
        along_y,
        along_z,
        square - 1.5,
        along_x * along_y,
        along_x * along_z,
        along_y * along_z,
        along_x * along_x - along_y * along_y,
        along_y * along_y - along_z * along_z,
        along_x * heat_term,
        along_y * heat_term,
        along_z * heat_term,
    ]
    stacked = np.stack(functions)
    basis = stacked / np.sqrt(np.mean(stacked * stacked, axis=(1, 2), keepdims=True))
    weights = np.exp(-square) * (spacing * spacing * spacing) / math.pi**1.5
    recon = basis * weights[None]
    return node_line, basis, recon


def bf16_split(table, parts):
    rest = np.asarray(table, np.float64)
    pieces = []
    for _ in range(parts):
        piece = rest.astype(np.float32).astype(jnp.bfloat16).astype(np.float64)
        pieces.append(piece)
        rest = rest - piece
    return pieces


def on_device(cotangent, freq, ratio, coupling, wall, inlet, face_type):
    pair_count = cotangent.shape[1]
    node_count = cotangent.shape[2]
    cell_count = cotangent.shape[3]
    assert cell_count == NZ
    half = pair_count // 2
    moment_count = coupling.shape[2]
    species_count = lax.axis_size("species")

    node_line, basis, recon = velocity_tables(node_count)
    basis_k = np.transpose(basis, (0, 2, 1)).reshape(moment_count, node_count * pair_count)
    basis_parts = np.concatenate(bf16_split(basis_k, 3), axis=0)
    basis_parts = jnp.asarray(basis_parts.astype(jnp.bfloat16))
    weight_k = (recon[0] / basis[0]).T.reshape(-1).astype(np.float32)

    field_in = jnp.transpose(cotangent[0], (1, 0, 2))
    upper_in = field_in[:, half:, :]
    lower_in = field_in[:, :half, :]
    got_next = passed_along(upper_in, "space", -1)
    got_prev = passed_along(lower_in, "space", 1)

    open_cells = (1 - wall).astype(jnp.float32)
    keep_upper = open_cells * (1.0 - inlet.astype(jnp.float32))
    upward = (jnp.arange(pair_count) >= half)[None, :, None]
    keep = jnp.where(upward, keep_upper[None, None, :], open_cells[None, None, :])
    masked = field_in * keep.astype(jnp.bfloat16)
    parts = jnp.dot(
        basis_parts,
        masked.reshape(node_count * pair_count, cell_count),
        preferred_element_type=jnp.float32,
    )
    moments = parts[:moment_count] + parts[moment_count : 2 * moment_count] + parts[2 * moment_count :]

    species_index = lax.axis_index("species")
    row_k = lax.dynamic_index_in_dim(coupling, species_index, axis=0, keepdims=False)
    own_weight = lax.dynamic_index_in_dim(row_k, species_index, axis=0, keepdims=False)
    cross = own_weight[:, None] * moments
    for shift in range(1, species_count):
        source = (species_index - shift) % species_count
        other = passed_along(moments, "species", shift)
        weight = lax.dynamic_index_in_dim(row_k, source, axis=0, keepdims=False)
        cross = cross + weight[:, None] * other

    rows = 16
    assert moment_count + 2 < rows
    packet = jnp.concatenate(
        [
            cross,
            open_cells[None],
            keep_upper[None],
            jnp.zeros((rows - moment_count - 2, cell_count), jnp.float32),
        ],
        axis=0,
    )
    packet_next = passed_along(packet, "space", -1)
    packet_prev = passed_along(packet, "space", 1)

    rate_value = freq[0]
    scale_factor = courant_max * ratio[0] / node_reach
    line = jnp.asarray(node_line.astype(np.float32))
    pair_line = jnp.repeat(line, node_count)
    adv_x = jnp.abs(scale_factor * pair_line)
    adv_z = jnp.abs(scale_factor * line)
    columns = jnp.broadcast_to(
        jnp.stack([1.0 - adv_x, adv_x])[:, :, None], (2, pair_count, cell_count)
    )
    scalars = jnp.concatenate(
        [adv_z, jnp.zeros((31 - node_count,), jnp.float32), (1.0 - rate_value)[None]]
    )
    faces = face_type[:, 0]

    lanes = 128
    recon_halves = jnp.asarray(packed_recon(recon, rows, lanes))

    flip_rows = lax.broadcasted_iota(jnp.int32, (pair_count, pair_count), 0)
    flip_cols = lax.broadcasted_iota(jnp.int32, (pair_count, pair_count), 1)
    flip = (flip_rows + flip_cols == pair_count - 1).astype(jnp.bfloat16)

    partial = own_kernel(field_in, recon_halves, packet, columns, flip, scalars, faces)
    out = halo_kernel(
        partial, got_next, got_prev, recon_halves, packet_next, packet_prev,
        columns, scalars,
    )
    return jnp.transpose(out, (1, 0, 2))[None]


def packed_recon(recon, rows, lanes):
    moment_count, pair_count, node_count = recon.shape
    half = pair_count // 2
    table = np.transpose(recon, (2, 1, 0))
    parts = bf16_split(table, 3)
    order = [0, 0, 1, 0, 1, 2]
    packed = np.zeros((node_count, pair_count, lanes), np.float32)
    for block, part in enumerate(order):
        packed[:, :, block * rows : block * rows + moment_count] = parts[part]
    packed = packed.reshape(node_count, 2, half, lanes)
    return packed.astype(jnp.bfloat16)


def cross_matrix(packet, moment_count):
    rows = packet.shape[0]
    row = lax.broadcasted_iota(jnp.int32, packet.shape, 0)
    values = jnp.where(row < moment_count, packet, 0.0)
    c1 = values.astype(jnp.bfloat16)
    left = values - c1.astype(jnp.float32)
    c2 = left.astype(jnp.bfloat16)
    c3 = (left - c2.astype(jnp.float32)).astype(jnp.bfloat16)
    pad = jnp.zeros((128 - 6 * rows, packet.shape[1]), jnp.bfloat16)
    return jnp.concatenate([c1, c2, c1, c3, c2, c1, pad], axis=0)


def own_kernel(field_in, recon_halves, packet, columns, flip, scalars, faces):
    node_count, pair_count, cell_count = field_in.shape
    half = pair_count // 2
    steps = node_count // 2
    moment_count = packet.shape[0] - 3
    group = 5 if steps % 5 == 0 else 1
    blocks = steps // group

    def kernel(sc_ref, face_ref, cot_lo, cot_hi, rec_lo, rec_hi, pk_ref, col_ref, flip_ref, out_ref):
        b = pl.program_id(0)
        row = lax.broadcasted_iota(jnp.int32, (pair_count, cell_count), 0)
        lane = lax.broadcasted_iota(jnp.int32, (pair_count, cell_count), 1)
        pk = pk_ref[...]
        rate = sc_ref[31]
        keep = rate * jnp.where(row >= half, pk[moment_count + 1 : moment_count + 2, :], pk[moment_count : moment_count + 1, :])
        own = cross_matrix(pk, moment_count)
        base = col_ref[0]
        face_a = face_ref[0] == 1
        face_b = face_ref[1] == 1

        def relax(values, rec_ref, at):
            rebuilt = jnp.concatenate(
                [
                    jnp.dot(rec_ref[at, 0], own, preferred_element_type=jnp.float32),
                    jnp.dot(rec_ref[at, 1], own, preferred_element_type=jnp.float32),
                ],
                axis=0,
            )
            return (keep * values.astype(jnp.float32) + rebuilt).astype(jnp.bfloat16)

        def one(t, carry):
            u = group - 1 - t
            j = b * group + t
            relaxed_a = relax(cot_lo[t], rec_lo, t)
            relaxed_b = relax(cot_hi[u], rec_hi, u)
            edges = jnp.where(lane == 0, relaxed_b, relaxed_a)
            flipped = jnp.dot(flip_ref[...], edges, preferred_element_type=jnp.float32)
            edges32 = edges.astype(jnp.float32)
            source_a = jnp.where(face_a, flipped, edges32)
            source_b = jnp.where(face_b, flipped, edges32)
            ra = relaxed_a.astype(jnp.float32)
            rb = relaxed_b.astype(jnp.float32)
            near_a = jnp.where(lane == 0, source_a, pltpu.roll(ra, 1, 1))
            near_b = jnp.where(lane == cell_count - 1, source_b, pltpu.roll(rb, cell_count - 1, 1))
            zw_a = sc_ref[j]
            zw_b = sc_ref[node_count - 1 - j]
            out_ref[0, t] = (base - zw_a) * ra + zw_a * near_a
            out_ref[1, t] = (base - zw_b) * rb + zw_b * near_b
            return carry

        lax.fori_loop(0, group, one, 0)

    block = (group, pair_count, cell_count)
    smem = pl.BlockSpec(memory_space=pltpu.SMEM)
    in_specs = [
        smem,
        smem,
        pl.BlockSpec(block, lambda b: (b, 0, 0)),
        pl.BlockSpec(block, lambda b: (2 * blocks - 1 - b, 0, 0)),
        pl.BlockSpec((group, 2, half, recon_halves.shape[3]), lambda b: (b, 0, 0, 0)),
        pl.BlockSpec((group, 2, half, recon_halves.shape[3]), lambda b: (2 * blocks - 1 - b, 0, 0, 0)),
        pl.BlockSpec(packet.shape, lambda b: (0, 0)),
        pl.BlockSpec((1, pair_count, cell_count), lambda b: (0, 0, 0)),
        pl.BlockSpec(flip.shape, lambda b: (0, 0)),
    ]
    return pl.pallas_call(
        kernel,
        grid=(blocks,),
        in_specs=in_specs,
        out_specs=pl.BlockSpec((2,) + block, lambda b: (0, b, 0, 0)),
        out_shape=jax.ShapeDtypeStruct((2, steps, pair_count, cell_count), jnp.float32),
        compiler_params=pltpu.CompilerParams(
            dimension_semantics=("arbitrary",), vmem_limit_bytes=60 * 1024 * 1024
        ),
    )(scalars, faces, field_in, field_in, recon_halves, recon_halves, packet, columns, flip)


def halo_kernel(partial, got_next, got_prev, recon_halves, packet_next, packet_prev, columns, scalars):
    node_count, half, cell_count = got_next.shape
    pair_count = 2 * half
    steps = node_count // 2
    moment_count = packet_next.shape[0] - 3
    group = 5 if steps % 5 == 0 else 1
    blocks = node_count // group
    lower_blocks = steps // group

    def kernel(sc_ref, part_ref, nxt_ref, prv_ref, rec_ref, pn_ref, pp_ref, col_ref, out_ref):
        i = pl.program_id(0)
        rate = sc_ref[31]
        pn = pn_ref[...]
        pp = pp_ref[...]
        next_mat = cross_matrix(pn, moment_count)
        prev_mat = cross_matrix(pp, moment_count)
        keep_up = rate * pn[moment_count + 1 : moment_count + 2, :]
        keep_down = rate * pp[moment_count : moment_count + 1, :]
        side = col_ref[0]

        def run(mirrored):
            def one(t, carry):
                up = jnp.dot(rec_ref[t, 1], next_mat, preferred_element_type=jnp.float32)
                down = jnp.dot(rec_ref[t, 0], prev_mat, preferred_element_type=jnp.float32)
                up = (keep_up * nxt_ref[t].astype(jnp.float32) + up).astype(jnp.bfloat16)
                down = (keep_down * prv_ref[t].astype(jnp.float32) + down).astype(jnp.bfloat16)
                shifted = jnp.concatenate([down.astype(jnp.float32), up.astype(jnp.float32)], axis=0)
                part = part_ref[0, group - 1 - t] if mirrored else part_ref[0, t]
                out_ref[t] = (part + side * shifted).astype(jnp.bfloat16)
                return carry

            lax.fori_loop(0, group, one, 0)

        @pl.when(i < lower_blocks)
        def _():
            run(False)

        @pl.when(i >= lower_blocks)
        def _():
            run(True)

    block = (group, pair_count, cell_count)
    smem = pl.BlockSpec(memory_space=pltpu.SMEM)
    in_specs = [
        smem,
        pl.BlockSpec(
            (1,) + block,
            lambda i: (
                jnp.where(i < lower_blocks, 0, 1),
                jnp.where(i < lower_blocks, i, blocks - 1 - i),
                0,
                0,
            ),
        ),
        pl.BlockSpec((group, half, cell_count), lambda i: (i, 0, 0)),
        pl.BlockSpec((group, half, cell_count), lambda i: (i, 0, 0)),
        pl.BlockSpec((group, 2, half, recon_halves.shape[3]), lambda i: (i, 0, 0, 0)),
        pl.BlockSpec(packet_next.shape, lambda i: (0, 0)),
        pl.BlockSpec(packet_prev.shape, lambda i: (0, 0)),
        pl.BlockSpec((1, pair_count, cell_count), lambda i: (1, 0, 0)),
    ]
    return pl.pallas_call(
        kernel,
        grid=(blocks,),
        in_specs=in_specs,
        out_specs=pl.BlockSpec(block, lambda i: (i, 0, 0)),
        out_shape=jax.ShapeDtypeStruct((node_count, pair_count, cell_count), jnp.bfloat16),
        compiler_params=pltpu.CompilerParams(
            dimension_semantics=("arbitrary",), vmem_limit_bytes=60 * 1024 * 1024
        ),
    )(scalars, partial, got_next, got_prev, recon_halves, packet_next, packet_prev, columns)


def solution(mesh):
    in_specs = (
        P("species", None, None, "space"),
        P("species"),
        P("species"),
        P(),
        P("space"),
        P("space"),
        P(None, "space"),
    )
    out_specs = P("species", None, None, "space")

    return jax.shard_map(on_device, mesh=mesh, in_specs=in_specs, out_specs=out_specs, check_vma=False)
```

```python
import math

import numpy as np
import jax
import jax.numpy as jnp
from jax import lax
from jax.experimental import pallas as pl
from jax.experimental.pallas import tpu as pltpu
from jax.sharding import PartitionSpec as P


NZ = 128

courant_max = 0.45
node_reach = 2.85


def passed_along(value, axis, steps):
    count = lax.axis_size(axis)
    pairs = [(source, (source + steps) % count) for source in range(count)]
    return lax.ppermute(value, axis, pairs)


def velocity_tables(node_count):
    pair_count = node_count * node_count
    spacing = 2.0 * node_reach / (node_count - 1)
    node_line = (np.arange(node_count, dtype=np.float64) - 0.5 * (node_count - 1)) * spacing
    grid_shape = (pair_count, node_count)
    along_x = np.broadcast_to(np.repeat(node_line, node_count)[:, None], grid_shape)
    along_y = np.broadcast_to(np.tile(node_line, node_count)[:, None], grid_shape)
    along_z = np.broadcast_to(node_line[None, :], grid_shape)
    square = along_x * along_x + along_y * along_y + along_z * along_z
    heat_term = square - 2.5
    functions = [
        np.ones(grid_shape),
        along_x,
        along_y,
        along_z,
        square - 1.5,
        along_x * along_y,
        along_x * along_z,
        along_y * along_z,
        along_x * along_x - along_y * along_y,
        along_y * along_y - along_z * along_z,
        along_x * heat_term,
        along_y * heat_term,
        along_z * heat_term,
    ]
    stacked = np.stack(functions)
    basis = stacked / np.sqrt(np.mean(stacked * stacked, axis=(1, 2), keepdims=True))
    weights = np.exp(-square) * (spacing * spacing * spacing) / math.pi**1.5
    recon = basis * weights[None]
    return node_line, basis, recon


def bf16_split(table, parts):
    rest = np.asarray(table, np.float64)
    pieces = []
    for _ in range(parts):
        piece = rest.astype(np.float32).astype(jnp.bfloat16).astype(np.float64)
        pieces.append(piece)
        rest = rest - piece
    return pieces


def on_device(cotangent, freq, ratio, coupling, wall, inlet, face_type):
    pair_count = cotangent.shape[1]
    node_count = cotangent.shape[2]
    cell_count = cotangent.shape[3]
    assert cell_count == NZ
    half = pair_count // 2
    moment_count = coupling.shape[2]
    species_count = lax.axis_size("species")

    node_line, basis, recon = velocity_tables(node_count)
    basis_k = np.transpose(basis, (0, 2, 1)).reshape(moment_count, node_count * pair_count)
    basis_parts = np.concatenate(bf16_split(basis_k, 3), axis=0)
    basis_parts = jnp.asarray(basis_parts.astype(jnp.bfloat16))
    weight_k = (recon[0] / basis[0]).T.reshape(-1).astype(np.float32)

    field_in = jnp.transpose(cotangent[0], (1, 0, 2))
    upper_in = field_in[:, half:, :]
    lower_in = field_in[:, :half, :]
    got_next = passed_along(upper_in, "space", -1)
    got_prev = passed_along(lower_in, "space", 1)

    open_cells = (1 - wall).astype(jnp.float32)
    keep_upper = open_cells * (1.0 - inlet.astype(jnp.float32))
    upward = (jnp.arange(pair_count) >= half)[None, :, None]
    keep = jnp.where(upward, keep_upper[None, None, :], open_cells[None, None, :])
    masked = field_in * keep.astype(jnp.bfloat16)
    parts = jnp.dot(
        basis_parts,
        masked.reshape(node_count * pair_count, cell_count),
        preferred_element_type=jnp.float32,
    )
    moments = parts[:moment_count] + parts[moment_count : 2 * moment_count] + parts[2 * moment_count :]

    species_index = lax.axis_index("species")
    row_k = lax.dynamic_index_in_dim(coupling, species_index, axis=0, keepdims=False)
    own_weight = lax.dynamic_index_in_dim(row_k, species_index, axis=0, keepdims=False)
    cross = own_weight[:, None] * moments
    for shift in range(1, species_count):
        source = (species_index - shift) % species_count
        other = passed_along(moments, "species", shift)
        weight = lax.dynamic_index_in_dim(row_k, source, axis=0, keepdims=False)
        cross = cross + weight[:, None] * other

    rows = 16
    assert moment_count + 2 < rows
    packet = jnp.concatenate(
        [
            cross,
            open_cells[None],
            keep_upper[None],
            jnp.zeros((rows - moment_count - 2, cell_count), jnp.float32),
        ],
        axis=0,
    )
    packet_next = passed_along(packet, "space", -1)
    packet_prev = passed_along(packet, "space", 1)

    rate_value = freq[0]
    scale_factor = courant_max * ratio[0] / node_reach
    line = jnp.asarray(node_line.astype(np.float32))
    pair_line = jnp.repeat(line, node_count)
    adv_x = jnp.abs(scale_factor * pair_line)
    adv_z = jnp.abs(scale_factor * line)
    columns = jnp.broadcast_to(
        jnp.stack([1.0 - adv_x, adv_x])[:, :, None], (2, pair_count, cell_count)
    )
    scalars = jnp.concatenate(
        [adv_z, jnp.zeros((31 - node_count,), jnp.float32), (1.0 - rate_value)[None]]
    )
    faces = face_type[:, 0]

    lanes = 128
    recon_halves = jnp.asarray(packed_recon(recon, rows, lanes))

    flip_rows = lax.broadcasted_iota(jnp.int32, (pair_count, pair_count), 0)
    flip_cols = lax.broadcasted_iota(jnp.int32, (pair_count, pair_count), 1)
    flip = (flip_rows + flip_cols == pair_count - 1).astype(jnp.bfloat16)

    partial = own_kernel(field_in, recon_halves, packet, columns, flip, scalars, faces)
    out = halo_kernel(
        partial, got_next, got_prev, recon_halves, packet_next, packet_prev,
        columns, scalars,
    )
    return jnp.transpose(out, (1, 0, 2))[None]


def packed_recon(recon, rows, lanes):
    moment_count, pair_count, node_count = recon.shape
    half = pair_count // 2
    table = np.transpose(recon, (2, 1, 0))
    parts = bf16_split(table, 2)
    order = [0, 0, 1]
    packed = np.zeros((node_count, half, lanes), np.float32)
    for side in range(2):
        for block, part in enumerate(order):
            at = side * (lanes // 2) + block * rows
            packed[:, :, at : at + moment_count] = parts[part][:, side * half : (side + 1) * half]
    return packed.astype(jnp.bfloat16)


def cross_matrix(packet, moment_count, side):
    rows, cells = packet.shape
    row = lax.broadcasted_iota(jnp.int32, packet.shape, 0)
    values = jnp.where(row < moment_count, packet, 0.0)
    c1 = values.astype(jnp.bfloat16)
    c2 = (values - c1.astype(jnp.float32)).astype(jnp.bfloat16)
    gap = jnp.zeros((64 - 3 * rows, cells), jnp.bfloat16)
    lead = jnp.zeros((64, cells), jnp.bfloat16)
    pieces = [c1, c2, c1, gap]
    return jnp.concatenate([lead] + pieces if side else pieces + [lead], axis=0)


def own_kernel(field_in, recon_halves, packet, columns, flip, scalars, faces):
    node_count, pair_count, cell_count = field_in.shape
    half = pair_count // 2
    steps = node_count // 2
    moment_count = packet.shape[0] - 3
    group = 5 if steps % 5 == 0 else 1
    blocks = steps // group

    def kernel(sc_ref, face_ref, cot_lo, cot_hi, rec_lo, rec_hi, pk_ref, col_ref, flip_ref, out_ref):
        b = pl.program_id(0)
        row = lax.broadcasted_iota(jnp.int32, (pair_count, cell_count), 0)
        lane = lax.broadcasted_iota(jnp.int32, (pair_count, cell_count), 1)
        pk = pk_ref[...]
        rate = sc_ref[31]
        keep = rate * jnp.where(row >= half, pk[moment_count + 1 : moment_count + 2, :], pk[moment_count : moment_count + 1, :])
        own_lo = cross_matrix(pk, moment_count, 0)
        own_hi = cross_matrix(pk, moment_count, 1)
        base = col_ref[0]
        face_a = face_ref[0] == 1
        face_b = face_ref[1] == 1

        def relax(values, rec_ref, at):
            rec = rec_ref[at]
            rebuilt = jnp.concatenate(
                [
                    jnp.dot(rec, own_lo, preferred_element_type=jnp.float32),
                    jnp.dot(rec, own_hi, preferred_element_type=jnp.float32),
                ],
                axis=0,
            )
            return (keep * values.astype(jnp.float32) + rebuilt).astype(jnp.bfloat16)

        def one(t, carry):
            u = group - 1 - t
            j = b * group + t
            relaxed_a = relax(cot_lo[t], rec_lo, t)
            relaxed_b = relax(cot_hi[u], rec_hi, u)
            edges = jnp.where(lane == 0, relaxed_b, relaxed_a)
            flipped = jnp.dot(flip_ref[...], edges, preferred_element_type=jnp.float32)
            edges32 = edges.astype(jnp.float32)
            source_a = jnp.where(face_a, flipped, edges32)
            source_b = jnp.where(face_b, flipped, edges32)
            ra = relaxed_a.astype(jnp.float32)
            rb = relaxed_b.astype(jnp.float32)
            near_a = jnp.where(lane == 0, source_a, pltpu.roll(ra, 1, 1))
            near_b = jnp.where(lane == cell_count - 1, source_b, pltpu.roll(rb, cell_count - 1, 1))
            zw_a = sc_ref[j]
            zw_b = sc_ref[node_count - 1 - j]
            out_ref[0, t] = (base - zw_a) * ra + zw_a * near_a
            out_ref[1, t] = (base - zw_b) * rb + zw_b * near_b
            return carry

        lax.fori_loop(0, group, one, 0)

    block = (group, pair_count, cell_count)
    smem = pl.BlockSpec(memory_space=pltpu.SMEM)
    in_specs = [
        smem,
        smem,
        pl.BlockSpec(block, lambda b: (b, 0, 0)),
        pl.BlockSpec(block, lambda b: (2 * blocks - 1 - b, 0, 0)),
        pl.BlockSpec((group, half, recon_halves.shape[2]), lambda b: (b, 0, 0)),
        pl.BlockSpec((group, half, recon_halves.shape[2]), lambda b: (2 * blocks - 1 - b, 0, 0)),
        pl.BlockSpec(packet.shape, lambda b: (0, 0)),
        pl.BlockSpec((1, pair_count, cell_count), lambda b: (0, 0, 0)),
        pl.BlockSpec(flip.shape, lambda b: (0, 0)),
    ]
    return pl.pallas_call(
        kernel,
        grid=(blocks,),
        in_specs=in_specs,
        out_specs=pl.BlockSpec((2,) + block, lambda b: (0, b, 0, 0)),
        out_shape=jax.ShapeDtypeStruct((2, steps, pair_count, cell_count), jnp.float32),
        compiler_params=pltpu.CompilerParams(
            dimension_semantics=("arbitrary",), vmem_limit_bytes=60 * 1024 * 1024
        ),
    )(scalars, faces, field_in, field_in, recon_halves, recon_halves, packet, columns, flip)


def halo_kernel(partial, got_next, got_prev, recon_halves, packet_next, packet_prev, columns, scalars):
    node_count, half, cell_count = got_next.shape
    pair_count = 2 * half
    steps = node_count // 2
    moment_count = packet_next.shape[0] - 3
    group = 5 if steps % 5 == 0 else 1
    blocks = node_count // group
    lower_blocks = steps // group

    def kernel(sc_ref, part_ref, nxt_ref, prv_ref, rec_ref, pn_ref, pp_ref, col_ref, out_ref):
        i = pl.program_id(0)
        rate = sc_ref[31]
        pn = pn_ref[...]
        pp = pp_ref[...]
        next_mat = cross_matrix(pn, moment_count, 1)
        prev_mat = cross_matrix(pp, moment_count, 0)
        keep_up = rate * pn[moment_count + 1 : moment_count + 2, :]
        keep_down = rate * pp[moment_count : moment_count + 1, :]
        side = col_ref[0]

        def run(mirrored):
            def one(t, carry):
                rec = rec_ref[t]
                up = jnp.dot(rec, next_mat, preferred_element_type=jnp.float32)
                down = jnp.dot(rec, prev_mat, preferred_element_type=jnp.float32)
                up = (keep_up * nxt_ref[t].astype(jnp.float32) + up).astype(jnp.bfloat16)
                down = (keep_down * prv_ref[t].astype(jnp.float32) + down).astype(jnp.bfloat16)
                shifted = jnp.concatenate([down.astype(jnp.float32), up.astype(jnp.float32)], axis=0)
                part = part_ref[0, group - 1 - t] if mirrored else part_ref[0, t]
                out_ref[t] = (part + side * shifted).astype(jnp.bfloat16)
                return carry

            lax.fori_loop(0, group, one, 0)

        @pl.when(i < lower_blocks)
        def _():
            run(False)

        @pl.when(i >= lower_blocks)
        def _():
            run(True)

    block = (group, pair_count, cell_count)
    smem = pl.BlockSpec(memory_space=pltpu.SMEM)
    in_specs = [
        smem,
        pl.BlockSpec(
            (1,) + block,
            lambda i: (
                jnp.where(i < lower_blocks, 0, 1),
                jnp.where(i < lower_blocks, i, blocks - 1 - i),
                0,
                0,
            ),
        ),
        pl.BlockSpec((group, half, cell_count), lambda i: (i, 0, 0)),
        pl.BlockSpec((group, half, cell_count), lambda i: (i, 0, 0)),
        pl.BlockSpec((group, half, recon_halves.shape[2]), lambda i: (i, 0, 0)),
        pl.BlockSpec(packet_next.shape, lambda i: (0, 0)),
        pl.BlockSpec(packet_prev.shape, lambda i: (0, 0)),
        pl.BlockSpec((1, pair_count, cell_count), lambda i: (1, 0, 0)),
    ]
    return pl.pallas_call(
        kernel,
        grid=(blocks,),
        in_specs=in_specs,
        out_specs=pl.BlockSpec(block, lambda i: (i, 0, 0)),
        out_shape=jax.ShapeDtypeStruct((node_count, pair_count, cell_count), jnp.bfloat16),
        compiler_params=pltpu.CompilerParams(
            dimension_semantics=("arbitrary",), vmem_limit_bytes=60 * 1024 * 1024
        ),
    )(scalars, partial, got_next, got_prev, recon_halves, packet_next, packet_prev, columns)


def solution(mesh):
    in_specs = (
        P("species", None, None, "space"),
        P("species"),
        P("species"),
        P(),
        P("space"),
        P("space"),
        P(None, "space"),
    )
    out_specs = P("species", None, None, "space")

    return jax.shard_map(on_device, mesh=mesh, in_specs=in_specs, out_specs=out_specs, check_vma=False)
```

```python
import math

import numpy as np
import jax
import jax.numpy as jnp
from jax import lax
from jax.experimental import pallas as pl
from jax.experimental.pallas import tpu as pltpu
from jax.sharding import PartitionSpec as P


NZ = 128

courant_max = 0.45
node_reach = 2.85


def passed_along(value, axis, steps):
    count = lax.axis_size(axis)
    pairs = [(source, (source + steps) % count) for source in range(count)]
    return lax.ppermute(value, axis, pairs)


def velocity_tables(node_count):
    pair_count = node_count * node_count
    spacing = 2.0 * node_reach / (node_count - 1)
    node_line = (np.arange(node_count, dtype=np.float64) - 0.5 * (node_count - 1)) * spacing
    grid_shape = (pair_count, node_count)
    along_x = np.broadcast_to(np.repeat(node_line, node_count)[:, None], grid_shape)
    along_y = np.broadcast_to(np.tile(node_line, node_count)[:, None], grid_shape)
    along_z = np.broadcast_to(node_line[None, :], grid_shape)
    square = along_x * along_x + along_y * along_y + along_z * along_z
    heat_term = square - 2.5
    functions = [
        np.ones(grid_shape),
        along_x,
        along_y,
        along_z,
        square - 1.5,
        along_x * along_y,
        along_x * along_z,
        along_y * along_z,
        along_x * along_x - along_y * along_y,
        along_y * along_y - along_z * along_z,
        along_x * heat_term,
        along_y * heat_term,
        along_z * heat_term,
    ]
    stacked = np.stack(functions)
    basis = stacked / np.sqrt(np.mean(stacked * stacked, axis=(1, 2), keepdims=True))
    weights = np.exp(-square) * (spacing * spacing * spacing) / math.pi**1.5
    recon = basis * weights[None]
    return node_line, basis, recon


def bf16_split(table, parts):
    rest = np.asarray(table, np.float64)
    pieces = []
    for _ in range(parts):
        piece = rest.astype(np.float32).astype(jnp.bfloat16).astype(np.float64)
        pieces.append(piece)
        rest = rest - piece
    return pieces


def on_device(cotangent, freq, ratio, coupling, wall, inlet, face_type):
    pair_count = cotangent.shape[1]
    node_count = cotangent.shape[2]
    cell_count = cotangent.shape[3]
    assert cell_count == NZ
    half = pair_count // 2
    moment_count = coupling.shape[2]
    species_count = lax.axis_size("species")

    node_line, basis, recon = velocity_tables(node_count)
    basis_k = np.transpose(basis, (0, 2, 1)).reshape(moment_count, node_count * pair_count)
    basis_parts = np.concatenate(bf16_split(basis_k, 3), axis=0)
    basis_parts = jnp.asarray(basis_parts.astype(jnp.bfloat16))
    weight_k = (recon[0] / basis[0]).T.reshape(-1).astype(np.float32)

    field_in = jnp.transpose(cotangent[0], (1, 0, 2))
    margin = (-half) % 16
    upper_in, lower_in = split_halves(field_in, half - margin, half + margin)
    got_next = passed_along(upper_in, "space", -1)
    got_prev = passed_along(lower_in, "space", 1)

    open_cells = (1 - wall).astype(jnp.float32)
    keep_upper = open_cells * (1.0 - inlet.astype(jnp.float32))
    upward = (jnp.arange(pair_count) >= half)[None, :, None]
    keep = jnp.where(upward, keep_upper[None, None, :], open_cells[None, None, :])
    masked = field_in * keep.astype(jnp.bfloat16)
    parts = jnp.dot(
        basis_parts,
        masked.reshape(node_count * pair_count, cell_count),
        preferred_element_type=jnp.float32,
    )
    moments = parts[:moment_count] + parts[moment_count : 2 * moment_count] + parts[2 * moment_count :]

    species_index = lax.axis_index("species")
    row_k = lax.dynamic_index_in_dim(coupling, species_index, axis=0, keepdims=False)
    own_weight = lax.dynamic_index_in_dim(row_k, species_index, axis=0, keepdims=False)
    cross = own_weight[:, None] * moments
    for shift in range(1, species_count):
        source = (species_index - shift) % species_count
        other = passed_along(moments, "species", shift)
        weight = lax.dynamic_index_in_dim(row_k, source, axis=0, keepdims=False)
        cross = cross + weight[:, None] * other

    rows = 16
    assert moment_count + 2 < rows
    packet = jnp.concatenate(
        [
            cross,
            open_cells[None],
            keep_upper[None],
            jnp.zeros((rows - moment_count - 2, cell_count), jnp.float32),
        ],
        axis=0,
    )
    packet_next = passed_along(packet, "space", -1)
    packet_prev = passed_along(packet, "space", 1)

    rate_value = freq[0]
    scale_factor = courant_max * ratio[0] / node_reach
    line = jnp.asarray(node_line.astype(np.float32))
    pair_line = jnp.repeat(line, node_count)
    adv_x = jnp.abs(scale_factor * pair_line)
    adv_z = jnp.abs(scale_factor * line)
    columns = jnp.broadcast_to(
        jnp.stack([1.0 - adv_x, adv_x])[:, :, None], (2, pair_count, cell_count)
    )
    scalars = jnp.concatenate(
        [adv_z, jnp.zeros((31 - node_count,), jnp.float32), (1.0 - rate_value)[None]]
    )
    faces = face_type[:, 0]

    lanes = 128
    recon_halves = jnp.asarray(packed_recon(recon, rows, lanes))

    flip_rows = lax.broadcasted_iota(jnp.int32, (pair_count, pair_count), 0)
    flip_cols = lax.broadcasted_iota(jnp.int32, (pair_count, pair_count), 1)
    flip = (flip_rows + flip_cols == pair_count - 1).astype(jnp.bfloat16)

    partial = own_kernel(field_in, recon_halves, packet, columns, flip, scalars, faces)
    out = halo_kernel(
        partial, got_next, got_prev, recon_halves, packet_next, packet_prev,
        columns, scalars,
    )
    return jnp.transpose(out, (1, 0, 2))[None]


def packed_recon(recon, rows, lanes):
    moment_count, pair_count, node_count = recon.shape
    half = pair_count // 2
    table = np.transpose(recon, (2, 1, 0))
    parts = bf16_split(table, 2)
    order = [0, 0, 1]
    packed = np.zeros((node_count, half, lanes), np.float32)
    for side in range(2):
        for block, part in enumerate(order):
            at = side * (lanes // 2) + block * rows
            packed[:, :, at : at + moment_count] = parts[part][:, side * half : (side + 1) * half]
    return packed.astype(jnp.bfloat16)


def split_halves(field_in, start, wide):
    node_count, _, cell_count = field_in.shape

    def kernel(x_hbm, up_hbm, lo_hbm, sems):
        up = pltpu.make_async_copy(x_hbm.at[:, pl.ds(start, wide), :], up_hbm, sems.at[0])
        lo = pltpu.make_async_copy(x_hbm.at[:, pl.ds(0, wide), :], lo_hbm, sems.at[1])
        up.start()
        lo.start()
        up.wait()
        lo.wait()

    shape = jax.ShapeDtypeStruct((node_count, wide, cell_count), field_in.dtype)
    any_space = pl.BlockSpec(memory_space=pl.ANY)
    return pl.pallas_call(
        kernel,
        in_specs=[any_space],
        out_specs=[any_space, any_space],
        out_shape=[shape, shape],
        scratch_shapes=[pltpu.SemaphoreType.DMA((2,))],
    )(field_in)


def cross_matrix(packet, moment_count, side):
    rows, cells = packet.shape
    row = lax.broadcasted_iota(jnp.int32, packet.shape, 0)
    values = jnp.where(row < moment_count, packet, 0.0)
    c1 = values.astype(jnp.bfloat16)
    c2 = (values - c1.astype(jnp.float32)).astype(jnp.bfloat16)
    gap = jnp.zeros((64 - 3 * rows, cells), jnp.bfloat16)
    lead = jnp.zeros((64, cells), jnp.bfloat16)
    pieces = [c1, c2, c1, gap]
    return jnp.concatenate([lead] + pieces if side else pieces + [lead], axis=0)


def own_kernel(field_in, recon_halves, packet, columns, flip, scalars, faces):
    node_count, pair_count, cell_count = field_in.shape
    half = pair_count // 2
    steps = node_count // 2
    moment_count = packet.shape[0] - 3
    group = 5 if steps % 5 == 0 else 1
    blocks = steps // group

    def kernel(sc_ref, face_ref, cot_lo, cot_hi, rec_lo, rec_hi, pk_ref, col_ref, flip_ref, out_ref):
        b = pl.program_id(0)
        row = lax.broadcasted_iota(jnp.int32, (pair_count, cell_count), 0)
        lane = lax.broadcasted_iota(jnp.int32, (pair_count, cell_count), 1)
        pk = pk_ref[...]
        rate = sc_ref[31]
        keep = rate * jnp.where(row >= half, pk[moment_count + 1 : moment_count + 2, :], pk[moment_count : moment_count + 1, :])
        own_lo = cross_matrix(pk, moment_count, 0)
        own_hi = cross_matrix(pk, moment_count, 1)
        base = col_ref[0]
        face_a = face_ref[0] == 1
        face_b = face_ref[1] == 1

        def relax(values, rec_ref, at):
            rec = rec_ref[at]
            rebuilt = jnp.concatenate(
                [
                    jnp.dot(rec, own_lo, preferred_element_type=jnp.float32),
                    jnp.dot(rec, own_hi, preferred_element_type=jnp.float32),
                ],
                axis=0,
            )
            return (keep * values.astype(jnp.float32) + rebuilt).astype(jnp.bfloat16)

        def one(t, carry):
            u = group - 1 - t
            j = b * group + t
            relaxed_a = relax(cot_lo[t], rec_lo, t)
            relaxed_b = relax(cot_hi[u], rec_hi, u)
            edges = jnp.where(lane == 0, relaxed_b, relaxed_a)
            flipped = jnp.dot(flip_ref[...], edges, preferred_element_type=jnp.float32)
            edges32 = edges.astype(jnp.float32)
            source_a = jnp.where(face_a, flipped, edges32)
            source_b = jnp.where(face_b, flipped, edges32)
            ra = relaxed_a.astype(jnp.float32)
            rb = relaxed_b.astype(jnp.float32)
            near_a = jnp.where(lane == 0, source_a, pltpu.roll(ra, 1, 1))
            near_b = jnp.where(lane == cell_count - 1, source_b, pltpu.roll(rb, cell_count - 1, 1))
            zw_a = sc_ref[j]
            zw_b = sc_ref[node_count - 1 - j]
            out_ref[0, t] = (base - zw_a) * ra + zw_a * near_a
            out_ref[1, t] = (base - zw_b) * rb + zw_b * near_b
            return carry

        lax.fori_loop(0, group, one, 0)

    block = (group, pair_count, cell_count)
    smem = pl.BlockSpec(memory_space=pltpu.SMEM)
    in_specs = [
        smem,
        smem,
        pl.BlockSpec(block, lambda b: (b, 0, 0)),
        pl.BlockSpec(block, lambda b: (2 * blocks - 1 - b, 0, 0)),
        pl.BlockSpec((group, half, recon_halves.shape[2]), lambda b: (b, 0, 0)),
        pl.BlockSpec((group, half, recon_halves.shape[2]), lambda b: (2 * blocks - 1 - b, 0, 0)),
        pl.BlockSpec(packet.shape, lambda b: (0, 0)),
        pl.BlockSpec((1, pair_count, cell_count), lambda b: (0, 0, 0)),
        pl.BlockSpec(flip.shape, lambda b: (0, 0)),
    ]
    return pl.pallas_call(
        kernel,
        grid=(blocks,),
        in_specs=in_specs,
        out_specs=pl.BlockSpec((2,) + block, lambda b: (0, b, 0, 0)),
        out_shape=jax.ShapeDtypeStruct((2, steps, pair_count, cell_count), jnp.float32),
        compiler_params=pltpu.CompilerParams(
            dimension_semantics=("arbitrary",), vmem_limit_bytes=60 * 1024 * 1024
        ),
    )(scalars, faces, field_in, field_in, recon_halves, recon_halves, packet, columns, flip)


def halo_kernel(partial, got_next, got_prev, recon_halves, packet_next, packet_prev, columns, scalars):
    node_count, wide, cell_count = got_next.shape
    half = recon_halves.shape[1]
    margin = wide - half
    pair_count = 2 * half
    steps = node_count // 2
    moment_count = packet_next.shape[0] - 3
    group = 5 if steps % 5 == 0 else 1
    blocks = node_count // group
    lower_blocks = steps // group

    def kernel(sc_ref, part_ref, nxt_ref, prv_ref, rec_ref, pn_ref, pp_ref, col_ref, out_ref):
        i = pl.program_id(0)
        rate = sc_ref[31]
        pn = pn_ref[...]
        pp = pp_ref[...]
        next_mat = cross_matrix(pn, moment_count, 1)
        prev_mat = cross_matrix(pp, moment_count, 0)
        keep_up = rate * pn[moment_count + 1 : moment_count + 2, :]
        keep_down = rate * pp[moment_count : moment_count + 1, :]
        side = col_ref[0]

        def run(mirrored):
            def one(t, carry):
                rec = rec_ref[t]
                up = jnp.dot(rec, next_mat, preferred_element_type=jnp.float32)
                down = jnp.dot(rec, prev_mat, preferred_element_type=jnp.float32)
                nxt = nxt_ref[t].astype(jnp.float32)[margin:]
                prv = prv_ref[t].astype(jnp.float32)[:half]
                up = (keep_up * nxt + up).astype(jnp.bfloat16)
                down = (keep_down * prv + down).astype(jnp.bfloat16)
                shifted = jnp.concatenate([down.astype(jnp.float32), up.astype(jnp.float32)], axis=0)
                part = part_ref[0, group - 1 - t] if mirrored else part_ref[0, t]
                out_ref[t] = (part + side * shifted).astype(jnp.bfloat16)
                return carry

            lax.fori_loop(0, group, one, 0)

        @pl.when(i < lower_blocks)
        def _():
            run(False)

        @pl.when(i >= lower_blocks)
        def _():
            run(True)

    block = (group, pair_count, cell_count)
    smem = pl.BlockSpec(memory_space=pltpu.SMEM)
    in_specs = [
        smem,
        pl.BlockSpec(
            (1,) + block,
            lambda i: (
                jnp.where(i < lower_blocks, 0, 1),
                jnp.where(i < lower_blocks, i, blocks - 1 - i),
                0,
                0,
            ),
        ),
        pl.BlockSpec((group, wide, cell_count), lambda i: (i, 0, 0)),
        pl.BlockSpec((group, wide, cell_count), lambda i: (i, 0, 0)),
        pl.BlockSpec((group, half, recon_halves.shape[2]), lambda i: (i, 0, 0)),
        pl.BlockSpec(packet_next.shape, lambda i: (0, 0)),
        pl.BlockSpec(packet_prev.shape, lambda i: (0, 0)),
        pl.BlockSpec((1, pair_count, cell_count), lambda i: (1, 0, 0)),
    ]
    return pl.pallas_call(
        kernel,
        grid=(blocks,),
        in_specs=in_specs,
        out_specs=pl.BlockSpec(block, lambda i: (i, 0, 0)),
        out_shape=jax.ShapeDtypeStruct((node_count, pair_count, cell_count), jnp.bfloat16),
        compiler_params=pltpu.CompilerParams(
            dimension_semantics=("arbitrary",), vmem_limit_bytes=60 * 1024 * 1024
        ),
    )(scalars, partial, got_next, got_prev, recon_halves, packet_next, packet_prev, columns)


def solution(mesh):
    in_specs = (
        P("species", None, None, "space"),
        P("species"),
        P("species"),
        P(),
        P("space"),
        P("space"),
        P(None, "space"),
    )
    out_specs = P("species", None, None, "space")

    return jax.shard_map(on_device, mesh=mesh, in_specs=in_specs, out_specs=out_specs, check_vma=False)
```

```python
import math

import numpy as np
import jax
import jax.numpy as jnp
from jax import lax
from jax.experimental import pallas as pl
from jax.experimental.pallas import tpu as pltpu
from jax.sharding import PartitionSpec as P


NZ = 128

courant_max = 0.45
node_reach = 2.85


def passed_along(value, axis, steps):
    count = lax.axis_size(axis)
    pairs = [(source, (source + steps) % count) for source in range(count)]
    return lax.ppermute(value, axis, pairs)


def velocity_tables(node_count):
    pair_count = node_count * node_count
    spacing = 2.0 * node_reach / (node_count - 1)
    node_line = (np.arange(node_count, dtype=np.float64) - 0.5 * (node_count - 1)) * spacing
    grid_shape = (pair_count, node_count)
    along_x = np.broadcast_to(np.repeat(node_line, node_count)[:, None], grid_shape)
    along_y = np.broadcast_to(np.tile(node_line, node_count)[:, None], grid_shape)
    along_z = np.broadcast_to(node_line[None, :], grid_shape)
    square = along_x * along_x + along_y * along_y + along_z * along_z
    heat_term = square - 2.5
    functions = [
        np.ones(grid_shape),
        along_x,
        along_y,
        along_z,
        square - 1.5,
        along_x * along_y,
        along_x * along_z,
        along_y * along_z,
        along_x * along_x - along_y * along_y,
        along_y * along_y - along_z * along_z,
        along_x * heat_term,
        along_y * heat_term,
        along_z * heat_term,
    ]
    stacked = np.stack(functions)
    basis = stacked / np.sqrt(np.mean(stacked * stacked, axis=(1, 2), keepdims=True))
    weights = np.exp(-square) * (spacing * spacing * spacing) / math.pi**1.5
    recon = basis * weights[None]
    return node_line, basis, recon


def bf16_split(table, parts):
    rest = np.asarray(table, np.float64)
    pieces = []
    for _ in range(parts):
        piece = rest.astype(np.float32).astype(jnp.bfloat16).astype(np.float64)
        pieces.append(piece)
        rest = rest - piece
    return pieces


def on_device(cotangent, freq, ratio, coupling, wall, inlet, face_type):
    pair_count = cotangent.shape[1]
    node_count = cotangent.shape[2]
    cell_count = cotangent.shape[3]
    assert cell_count == NZ
    half = pair_count // 2
    moment_count = coupling.shape[2]
    species_count = lax.axis_size("species")

    node_line, basis, recon = velocity_tables(node_count)
    basis_k = np.transpose(basis, (0, 2, 1)).reshape(moment_count, node_count * pair_count)
    basis_parts = np.concatenate(bf16_split(basis_k, 3), axis=0)
    basis_parts = jnp.asarray(basis_parts.astype(jnp.bfloat16))
    weight_k = (recon[0] / basis[0]).T.reshape(-1).astype(np.float32)

    field_in = jnp.transpose(cotangent[0], (1, 0, 2))
    margin = (-half) % 16
    upper_in = field_in[:, half - margin :, :]
    lower_in = field_in[:, : half + margin, :]
    got_next = passed_along(upper_in, "space", -1)
    got_prev = passed_along(lower_in, "space", 1)

    open_cells = (1 - wall).astype(jnp.float32)
    keep_upper = open_cells * (1.0 - inlet.astype(jnp.float32))
    upward = (jnp.arange(pair_count) >= half)[None, :, None]
    keep = jnp.where(upward, keep_upper[None, None, :], open_cells[None, None, :])
    masked = field_in * keep.astype(jnp.bfloat16)
    parts = jnp.dot(
        basis_parts,
        masked.reshape(node_count * pair_count, cell_count),
        preferred_element_type=jnp.float32,
    )
    moments = parts[:moment_count] + parts[moment_count : 2 * moment_count] + parts[2 * moment_count :]

    species_index = lax.axis_index("species")
    row_k = lax.dynamic_index_in_dim(coupling, species_index, axis=0, keepdims=False)
    own_weight = lax.dynamic_index_in_dim(row_k, species_index, axis=0, keepdims=False)
    cross = own_weight[:, None] * moments
    for shift in range(1, species_count):
        source = (species_index - shift) % species_count
        other = passed_along(moments, "species", shift)
        weight = lax.dynamic_index_in_dim(row_k, source, axis=0, keepdims=False)
        cross = cross + weight[:, None] * other

    rows = 16
    assert moment_count + 2 < rows
    packet = jnp.concatenate(
        [
            cross,
            open_cells[None],
            keep_upper[None],
            jnp.zeros((rows - moment_count - 2, cell_count), jnp.float32),
        ],
        axis=0,
    )
    packet_next = passed_along(packet, "space", -1)
    packet_prev = passed_along(packet, "space", 1)

    rate_value = freq[0]
    scale_factor = courant_max * ratio[0] / node_reach
    line = jnp.asarray(node_line.astype(np.float32))
    pair_line = jnp.repeat(line, node_count)
    adv_x = jnp.abs(scale_factor * pair_line)
    adv_z = jnp.abs(scale_factor * line)
    columns = jnp.broadcast_to(
        jnp.stack([1.0 - adv_x, adv_x])[:, :, None], (2, pair_count, cell_count)
    )
    scalars = jnp.concatenate(
        [adv_z, jnp.zeros((31 - node_count,), jnp.float32), (1.0 - rate_value)[None]]
    )
    faces = face_type[:, 0]

    lanes = 128
    recon_halves = jnp.asarray(packed_recon(recon, rows, lanes))

    flip_rows = lax.broadcasted_iota(jnp.int32, (pair_count, pair_count), 0)
    flip_cols = lax.broadcasted_iota(jnp.int32, (pair_count, pair_count), 1)
    flip = (flip_rows + flip_cols == pair_count - 1).astype(jnp.bfloat16)

    partial = own_kernel(field_in, recon_halves, packet, columns, flip, scalars, faces)
    out = halo_kernel(
        partial, got_next, got_prev, recon_halves, packet_next, packet_prev,
        columns, scalars,
    )
    return jnp.transpose(out, (1, 0, 2))[None]


def packed_recon(recon, rows, lanes):
    moment_count, pair_count, node_count = recon.shape
    half = pair_count // 2
    table = np.transpose(recon, (2, 1, 0))
    parts = bf16_split(table, 2)
    order = [0, 0, 1]
    packed = np.zeros((node_count, half, lanes), np.float32)
    for side in range(2):
        for block, part in enumerate(order):
            at = side * (lanes // 2) + block * rows
            packed[:, :, at : at + moment_count] = parts[part][:, side * half : (side + 1) * half]
    return packed.astype(jnp.bfloat16)


def cross_matrix(packet, moment_count, side):
    rows, cells = packet.shape
    row = lax.broadcasted_iota(jnp.int32, packet.shape, 0)
    values = jnp.where(row < moment_count, packet, 0.0)
    c1 = values.astype(jnp.bfloat16)
    c2 = (values - c1.astype(jnp.float32)).astype(jnp.bfloat16)
    gap = jnp.zeros((64 - 3 * rows, cells), jnp.bfloat16)
    lead = jnp.zeros((64, cells), jnp.bfloat16)
    pieces = [c1, c2, c1, gap]
    return jnp.concatenate([lead] + pieces if side else pieces + [lead], axis=0)


def own_kernel(field_in, recon_halves, packet, columns, flip, scalars, faces):
    node_count, pair_count, cell_count = field_in.shape
    half = pair_count // 2
    steps = node_count // 2
    moment_count = packet.shape[0] - 3
    group = 5 if steps % 5 == 0 else 1
    blocks = steps // group

    def kernel(sc_ref, face_ref, cot_lo, cot_hi, rec_lo, rec_hi, pk_ref, col_ref, flip_ref, out_ref):
        b = pl.program_id(0)
        row = lax.broadcasted_iota(jnp.int32, (pair_count, cell_count), 0)
        lane = lax.broadcasted_iota(jnp.int32, (pair_count, cell_count), 1)
        pk = pk_ref[...]
        rate = sc_ref[31]
        keep = rate * jnp.where(row >= half, pk[moment_count + 1 : moment_count + 2, :], pk[moment_count : moment_count + 1, :])
        own_lo = cross_matrix(pk, moment_count, 0)
        own_hi = cross_matrix(pk, moment_count, 1)
        base = col_ref[0]
        face_a = face_ref[0] == 1
        face_b = face_ref[1] == 1

        def relax(values, rec_ref, at):
            rec = rec_ref[at]
            rebuilt = jnp.concatenate(
                [
                    jnp.dot(rec, own_lo, preferred_element_type=jnp.float32),
                    jnp.dot(rec, own_hi, preferred_element_type=jnp.float32),
                ],
                axis=0,
            )
            return (keep * values.astype(jnp.float32) + rebuilt).astype(jnp.bfloat16)

        def one(t, carry):
            u = group - 1 - t
            j = b * group + t
            relaxed_a = relax(cot_lo[t], rec_lo, t)
            relaxed_b = relax(cot_hi[u], rec_hi, u)
            edges = jnp.where(lane == 0, relaxed_b, relaxed_a)
            flipped = jnp.dot(flip_ref[...], edges, preferred_element_type=jnp.float32)
            edges32 = edges.astype(jnp.float32)
            source_a = jnp.where(face_a, flipped, edges32)
            source_b = jnp.where(face_b, flipped, edges32)
            ra = relaxed_a.astype(jnp.float32)
            rb = relaxed_b.astype(jnp.float32)
            near_a = jnp.where(lane == 0, source_a, pltpu.roll(ra, 1, 1))
            near_b = jnp.where(lane == cell_count - 1, source_b, pltpu.roll(rb, cell_count - 1, 1))
            zw_a = sc_ref[j]
            zw_b = sc_ref[node_count - 1 - j]
            out_ref[0, t] = (base - zw_a) * ra + zw_a * near_a
            out_ref[1, t] = (base - zw_b) * rb + zw_b * near_b
            return carry

        lax.fori_loop(0, group, one, 0)

    block = (group, pair_count, cell_count)
    smem = pl.BlockSpec(memory_space=pltpu.SMEM)
    in_specs = [
        smem,
        smem,
        pl.BlockSpec(block, lambda b: (b, 0, 0)),
        pl.BlockSpec(block, lambda b: (2 * blocks - 1 - b, 0, 0)),
        pl.BlockSpec((group, half, recon_halves.shape[2]), lambda b: (b, 0, 0)),
        pl.BlockSpec((group, half, recon_halves.shape[2]), lambda b: (2 * blocks - 1 - b, 0, 0)),
        pl.BlockSpec(packet.shape, lambda b: (0, 0)),
        pl.BlockSpec((1, pair_count, cell_count), lambda b: (0, 0, 0)),
        pl.BlockSpec(flip.shape, lambda b: (0, 0)),
    ]
    return pl.pallas_call(
        kernel,
        grid=(blocks,),
        in_specs=in_specs,
        out_specs=pl.BlockSpec((2,) + block, lambda b: (0, b, 0, 0)),
        out_shape=jax.ShapeDtypeStruct((2, steps, pair_count, cell_count), jnp.float32),
        compiler_params=pltpu.CompilerParams(
            dimension_semantics=("arbitrary",), vmem_limit_bytes=48 * 1024 * 1024
        ),
    )(scalars, faces, field_in, field_in, recon_halves, recon_halves, packet, columns, flip)


def halo_kernel(partial, got_next, got_prev, recon_halves, packet_next, packet_prev, columns, scalars):
    node_count, wide, cell_count = got_next.shape
    half = recon_halves.shape[1]
    margin = wide - half
    pair_count = 2 * half
    steps = node_count // 2
    moment_count = packet_next.shape[0] - 3
    group = 5 if steps % 5 == 0 else 1
    blocks = node_count // group
    lower_blocks = steps // group

    def kernel(sc_ref, part_ref, nxt_ref, prv_ref, rec_ref, pn_ref, pp_ref, col_ref, out_ref):
        i = pl.program_id(0)
        rate = sc_ref[31]
        pn = pn_ref[...]
        pp = pp_ref[...]
        next_mat = cross_matrix(pn, moment_count, 1)
        prev_mat = cross_matrix(pp, moment_count, 0)
        keep_up = rate * pn[moment_count + 1 : moment_count + 2, :]
        keep_down = rate * pp[moment_count : moment_count + 1, :]
        side = col_ref[0]

        def run(mirrored):
            def one(t, carry):
                rec = rec_ref[t]
                up = jnp.dot(rec, next_mat, preferred_element_type=jnp.float32)
                down = jnp.dot(rec, prev_mat, preferred_element_type=jnp.float32)
                nxt = nxt_ref[t].astype(jnp.float32)[margin:]
                prv = prv_ref[t].astype(jnp.float32)[:half]
                up = (keep_up * nxt + up).astype(jnp.bfloat16)
                down = (keep_down * prv + down).astype(jnp.bfloat16)
                shifted = jnp.concatenate([down.astype(jnp.float32), up.astype(jnp.float32)], axis=0)
                part = part_ref[0, group - 1 - t] if mirrored else part_ref[0, t]
                out_ref[t] = (part + side * shifted).astype(jnp.bfloat16)
                return carry

            lax.fori_loop(0, group, one, 0)

        @pl.when(i < lower_blocks)
        def _():
            run(False)

        @pl.when(i >= lower_blocks)
        def _():
            run(True)

    block = (group, pair_count, cell_count)
    smem = pl.BlockSpec(memory_space=pltpu.SMEM)
    in_specs = [
        smem,
        pl.BlockSpec(
            (1,) + block,
            lambda i: (
                jnp.where(i < lower_blocks, 0, 1),
                jnp.where(i < lower_blocks, i, blocks - 1 - i),
                0,
                0,
            ),
        ),
        pl.BlockSpec((group, wide, cell_count), lambda i: (i, 0, 0)),
        pl.BlockSpec((group, wide, cell_count), lambda i: (i, 0, 0)),
        pl.BlockSpec((group, half, recon_halves.shape[2]), lambda i: (i, 0, 0)),
        pl.BlockSpec(packet_next.shape, lambda i: (0, 0)),
        pl.BlockSpec(packet_prev.shape, lambda i: (0, 0)),
        pl.BlockSpec((1, pair_count, cell_count), lambda i: (1, 0, 0)),
    ]
    return pl.pallas_call(
        kernel,
        grid=(blocks,),
        in_specs=in_specs,
        out_specs=pl.BlockSpec(block, lambda i: (i, 0, 0)),
        out_shape=jax.ShapeDtypeStruct((node_count, pair_count, cell_count), jnp.bfloat16),
        compiler_params=pltpu.CompilerParams(
            dimension_semantics=("arbitrary",), vmem_limit_bytes=48 * 1024 * 1024
        ),
    )(scalars, partial, got_next, got_prev, recon_halves, packet_next, packet_prev, columns)


def solution(mesh):
    in_specs = (
        P("species", None, None, "space"),
        P("species"),
        P("species"),
        P(),
        P("space"),
        P("space"),
        P(None, "space"),
    )
    out_specs = P("species", None, None, "space")

    return jax.shard_map(on_device, mesh=mesh, in_specs=in_specs, out_specs=out_specs, check_vma=False)
```

```python
import math

import numpy as np
import jax
import jax.numpy as jnp
from jax import lax
from jax.experimental import pallas as pl
from jax.experimental.pallas import tpu as pltpu
from jax.sharding import PartitionSpec as P


NZ = 128

courant_max = 0.45
node_reach = 2.85


def passed_along(value, axis, steps):
    count = lax.axis_size(axis)
    pairs = [(source, (source + steps) % count) for source in range(count)]
    return lax.ppermute(value, axis, pairs)


def velocity_tables(node_count):
    pair_count = node_count * node_count
    spacing = 2.0 * node_reach / (node_count - 1)
    node_line = (np.arange(node_count, dtype=np.float64) - 0.5 * (node_count - 1)) * spacing
    grid_shape = (pair_count, node_count)
    along_x = np.broadcast_to(np.repeat(node_line, node_count)[:, None], grid_shape)
    along_y = np.broadcast_to(np.tile(node_line, node_count)[:, None], grid_shape)
    along_z = np.broadcast_to(node_line[None, :], grid_shape)
    square = along_x * along_x + along_y * along_y + along_z * along_z
    heat_term = square - 2.5
    functions = [
        np.ones(grid_shape),
        along_x,
        along_y,
        along_z,
        square - 1.5,
        along_x * along_y,
        along_x * along_z,
        along_y * along_z,
        along_x * along_x - along_y * along_y,
        along_y * along_y - along_z * along_z,
        along_x * heat_term,
        along_y * heat_term,
        along_z * heat_term,
    ]
    stacked = np.stack(functions)
    basis = stacked / np.sqrt(np.mean(stacked * stacked, axis=(1, 2), keepdims=True))
    weights = np.exp(-square) * (spacing * spacing * spacing) / math.pi**1.5
    recon = basis * weights[None]
    return node_line, basis, recon


def bf16_split(table, parts):
    rest = np.asarray(table, np.float64)
    pieces = []
    for _ in range(parts):
        piece = rest.astype(np.float32).astype(jnp.bfloat16).astype(np.float64)
        pieces.append(piece)
        rest = rest - piece
    return pieces


def on_device(cotangent, freq, ratio, coupling, wall, inlet, face_type):
    pair_count = cotangent.shape[1]
    node_count = cotangent.shape[2]
    cell_count = cotangent.shape[3]
    assert cell_count == NZ
    half = pair_count // 2
    moment_count = coupling.shape[2]
    species_count = lax.axis_size("species")

    node_line, basis, recon = velocity_tables(node_count)
    basis_k = np.transpose(basis, (0, 2, 1)).reshape(moment_count, node_count * pair_count)
    basis_parts = np.concatenate(bf16_split(basis_k, 3), axis=0)
    basis_parts = jnp.asarray(basis_parts.astype(jnp.bfloat16))
    weight_k = (recon[0] / basis[0]).T.reshape(-1).astype(np.float32)

    field_in = jnp.transpose(cotangent[0], (1, 0, 2))
    margin = (-half) % 16
    upper_in = field_in[:, half - margin :, :]
    lower_in = field_in[:, : half + margin, :]
    got_next = passed_along(upper_in, "space", -1)
    got_prev = passed_along(lower_in, "space", 1)

    open_cells = (1 - wall).astype(jnp.float32)
    keep_upper = open_cells * (1.0 - inlet.astype(jnp.float32))
    upward = (jnp.arange(pair_count) >= half)[None, :, None]
    keep = jnp.where(upward, keep_upper[None, None, :], open_cells[None, None, :])
    masked = field_in * keep.astype(jnp.bfloat16)
    parts = jnp.dot(
        basis_parts,
        masked.reshape(node_count * pair_count, cell_count),
        preferred_element_type=jnp.float32,
    )
    moments = parts[:moment_count] + parts[moment_count : 2 * moment_count] + parts[2 * moment_count :]

    species_index = lax.axis_index("species")
    row_k = lax.dynamic_index_in_dim(coupling, species_index, axis=0, keepdims=False)
    own_weight = lax.dynamic_index_in_dim(row_k, species_index, axis=0, keepdims=False)
    cross = own_weight[:, None] * moments
    for shift in range(1, species_count):
        source = (species_index - shift) % species_count
        other = passed_along(moments, "species", shift)
        weight = lax.dynamic_index_in_dim(row_k, source, axis=0, keepdims=False)
        cross = cross + weight[:, None] * other

    rows = 16
    assert moment_count + 2 < rows
    packet = jnp.concatenate(
        [
            cross,
            open_cells[None],
            keep_upper[None],
            jnp.zeros((rows - moment_count - 2, cell_count), jnp.float32),
        ],
        axis=0,
    )
    packet_next = passed_along(packet, "space", -1)
    packet_prev = passed_along(packet, "space", 1)

    rate_value = freq[0]
    scale_factor = courant_max * ratio[0] / node_reach
    line = jnp.asarray(node_line.astype(np.float32))
    pair_line = jnp.repeat(line, node_count)
    adv_x = jnp.abs(scale_factor * pair_line)
    adv_z = jnp.abs(scale_factor * line)
    columns = jnp.broadcast_to(
        jnp.stack([1.0 - adv_x, adv_x])[:, :, None], (2, pair_count, cell_count)
    )
    scalars = jnp.concatenate(
        [adv_z, jnp.zeros((31 - node_count,), jnp.float32), (1.0 - rate_value)[None]]
    )
    faces = face_type[:, 0]

    lanes = 128
    recon_halves = jnp.asarray(packed_recon(recon, rows, lanes))

    flip_rows = lax.broadcasted_iota(jnp.int32, (pair_count, pair_count), 0)
    flip_cols = lax.broadcasted_iota(jnp.int32, (pair_count, pair_count), 1)
    flip = (flip_rows + flip_cols == pair_count - 1).astype(jnp.bfloat16)

    partial = own_kernel(field_in, recon_halves, packet, columns, flip, scalars, faces)
    out = halo_kernel(
        partial, got_next, got_prev, recon_halves, packet_next, packet_prev,
        columns, scalars,
    )
    return jnp.transpose(out, (1, 0, 2))[None]


def packed_recon(recon, rows, lanes):
    moment_count, pair_count, node_count = recon.shape
    half = pair_count // 2
    table = np.transpose(recon, (2, 1, 0))
    parts = bf16_split(table, 2)
    order = [0, 0, 1]
    packed = np.zeros((node_count, half, lanes), np.float32)
    for side in range(2):
        for block, part in enumerate(order):
            at = side * (lanes // 2) + block * rows
            packed[:, :, at : at + moment_count] = parts[part][:, side * half : (side + 1) * half]
    return packed.astype(jnp.bfloat16)


def cross_matrix(packet, moment_count, side):
    rows, cells = packet.shape
    row = lax.broadcasted_iota(jnp.int32, packet.shape, 0)
    values = jnp.where(row < moment_count, packet, 0.0)
    c1 = values.astype(jnp.bfloat16)
    c2 = (values - c1.astype(jnp.float32)).astype(jnp.bfloat16)
    gap = jnp.zeros((64 - 3 * rows, cells), jnp.bfloat16)
    lead = jnp.zeros((64, cells), jnp.bfloat16)
    pieces = [c1, c2, c1, gap]
    return jnp.concatenate([lead] + pieces if side else pieces + [lead], axis=0)


def own_kernel(field_in, recon_halves, packet, columns, flip, scalars, faces):
    node_count, pair_count, cell_count = field_in.shape
    half = pair_count // 2
    steps = node_count // 2
    moment_count = packet.shape[0] - 3
    group = 5 if steps % 5 == 0 else 1
    blocks = steps // group

    def kernel(sc_ref, face_ref, cot_lo, cot_hi, rec_lo, rec_hi, pk_ref, col_ref, flip_ref, out_ref):
        b = pl.program_id(0)
        row = lax.broadcasted_iota(jnp.int32, (pair_count, cell_count), 0)
        lane = lax.broadcasted_iota(jnp.int32, (pair_count, cell_count), 1)
        pk = pk_ref[...]
        rate = sc_ref[31]
        keep = rate * jnp.where(row >= half, pk[moment_count + 1 : moment_count + 2, :], pk[moment_count : moment_count + 1, :])
        own_both = jnp.concatenate(
            [cross_matrix(pk, moment_count, 0), cross_matrix(pk, moment_count, 1)], axis=1
        )
        base = col_ref[0]
        face_a = face_ref[0] == 1
        face_b = face_ref[1] == 1

        def relax(values, rec_ref, at):
            both = jnp.dot(rec_ref[at], own_both, preferred_element_type=jnp.float32)
            rebuilt = jnp.concatenate([both[:, :cell_count], both[:, cell_count:]], axis=0)
            return (keep * values.astype(jnp.float32) + rebuilt).astype(jnp.bfloat16)

        def one(t, carry):
            u = group - 1 - t
            j = b * group + t
            relaxed_a = relax(cot_lo[t], rec_lo, t)
            relaxed_b = relax(cot_hi[u], rec_hi, u)
            edges = jnp.where(lane == 0, relaxed_b, relaxed_a)
            flipped = jnp.dot(flip_ref[...], edges, preferred_element_type=jnp.float32)
            edges32 = edges.astype(jnp.float32)
            source_a = jnp.where(face_a, flipped, edges32)
            source_b = jnp.where(face_b, flipped, edges32)
            ra = relaxed_a.astype(jnp.float32)
            rb = relaxed_b.astype(jnp.float32)
            near_a = jnp.where(lane == 0, source_a, pltpu.roll(ra, 1, 1))
            near_b = jnp.where(lane == cell_count - 1, source_b, pltpu.roll(rb, cell_count - 1, 1))
            zw_a = sc_ref[j]
            zw_b = sc_ref[node_count - 1 - j]
            out_ref[0, t] = (base - zw_a) * ra + zw_a * near_a
            out_ref[1, t] = (base - zw_b) * rb + zw_b * near_b
            return carry

        lax.fori_loop(0, group, one, 0)

    block = (group, pair_count, cell_count)
    smem = pl.BlockSpec(memory_space=pltpu.SMEM)
    in_specs = [
        smem,
        smem,
        pl.BlockSpec(block, lambda b: (b, 0, 0)),
        pl.BlockSpec(block, lambda b: (2 * blocks - 1 - b, 0, 0)),
        pl.BlockSpec((group, half, recon_halves.shape[2]), lambda b: (b, 0, 0)),
        pl.BlockSpec((group, half, recon_halves.shape[2]), lambda b: (2 * blocks - 1 - b, 0, 0)),
        pl.BlockSpec(packet.shape, lambda b: (0, 0)),
        pl.BlockSpec((1, pair_count, cell_count), lambda b: (0, 0, 0)),
        pl.BlockSpec(flip.shape, lambda b: (0, 0)),
    ]
    return pl.pallas_call(
        kernel,
        grid=(blocks,),
        in_specs=in_specs,
        out_specs=pl.BlockSpec((2,) + block, lambda b: (0, b, 0, 0)),
        out_shape=jax.ShapeDtypeStruct((2, steps, pair_count, cell_count), jnp.float32),
        compiler_params=pltpu.CompilerParams(
            dimension_semantics=("arbitrary",), vmem_limit_bytes=48 * 1024 * 1024
        ),
    )(scalars, faces, field_in, field_in, recon_halves, recon_halves, packet, columns, flip)


def halo_kernel(partial, got_next, got_prev, recon_halves, packet_next, packet_prev, columns, scalars):
    node_count, wide, cell_count = got_next.shape
    half = recon_halves.shape[1]
    margin = wide - half
    pair_count = 2 * half
    steps = node_count // 2
    moment_count = packet_next.shape[0] - 3
    group = 5 if steps % 5 == 0 else 1
    blocks = node_count // group
    lower_blocks = steps // group

    def kernel(sc_ref, part_ref, nxt_ref, prv_ref, rec_ref, pn_ref, pp_ref, col_ref, out_ref):
        i = pl.program_id(0)
        rate = sc_ref[31]
        pn = pn_ref[...]
        pp = pp_ref[...]
        halo_mats = jnp.concatenate(
            [cross_matrix(pn, moment_count, 1), cross_matrix(pp, moment_count, 0)], axis=1
        )
        keep_up = rate * pn[moment_count + 1 : moment_count + 2, :]
        keep_down = rate * pp[moment_count : moment_count + 1, :]
        side = col_ref[0]

        def run(mirrored):
            def one(t, carry):
                both = jnp.dot(rec_ref[t], halo_mats, preferred_element_type=jnp.float32)
                up = both[:, :cell_count]
                down = both[:, cell_count:]
                nxt = nxt_ref[t].astype(jnp.float32)[margin:]
                prv = prv_ref[t].astype(jnp.float32)[:half]
                up = (keep_up * nxt + up).astype(jnp.bfloat16)
                down = (keep_down * prv + down).astype(jnp.bfloat16)
                shifted = jnp.concatenate([down.astype(jnp.float32), up.astype(jnp.float32)], axis=0)
                part = part_ref[0, group - 1 - t] if mirrored else part_ref[0, t]
                out_ref[t] = (part + side * shifted).astype(jnp.bfloat16)
                return carry

            lax.fori_loop(0, group, one, 0)

        @pl.when(i < lower_blocks)
        def _():
            run(False)

        @pl.when(i >= lower_blocks)
        def _():
            run(True)

    block = (group, pair_count, cell_count)
    smem = pl.BlockSpec(memory_space=pltpu.SMEM)
    in_specs = [
        smem,
        pl.BlockSpec(
            (1,) + block,
            lambda i: (
                jnp.where(i < lower_blocks, 0, 1),
                jnp.where(i < lower_blocks, i, blocks - 1 - i),
                0,
                0,
            ),
        ),
        pl.BlockSpec((group, wide, cell_count), lambda i: (i, 0, 0)),
        pl.BlockSpec((group, wide, cell_count), lambda i: (i, 0, 0)),
        pl.BlockSpec((group, half, recon_halves.shape[2]), lambda i: (i, 0, 0)),
        pl.BlockSpec(packet_next.shape, lambda i: (0, 0)),
        pl.BlockSpec(packet_prev.shape, lambda i: (0, 0)),
        pl.BlockSpec((1, pair_count, cell_count), lambda i: (1, 0, 0)),
    ]
    return pl.pallas_call(
        kernel,
        grid=(blocks,),
        in_specs=in_specs,
        out_specs=pl.BlockSpec(block, lambda i: (i, 0, 0)),
        out_shape=jax.ShapeDtypeStruct((node_count, pair_count, cell_count), jnp.bfloat16),
        compiler_params=pltpu.CompilerParams(
            dimension_semantics=("arbitrary",), vmem_limit_bytes=48 * 1024 * 1024
        ),
    )(scalars, partial, got_next, got_prev, recon_halves, packet_next, packet_prev, columns)


def solution(mesh):
    in_specs = (
        P("species", None, None, "space"),
        P("species"),
        P("species"),
        P(),
        P("space"),
        P("space"),
        P(None, "space"),
    )
    out_specs = P("species", None, None, "space")

    return jax.shard_map(on_device, mesh=mesh, in_specs=in_specs, out_specs=out_specs, check_vma=False)
```

```python
import math

import numpy as np
import jax
import jax.numpy as jnp
from jax import lax
from jax.experimental import pallas as pl
from jax.experimental.pallas import tpu as pltpu
from jax.sharding import PartitionSpec as P


NZ = 128

courant_max = 0.45
node_reach = 2.85


def passed_along(value, axis, steps):
    count = lax.axis_size(axis)
    pairs = [(source, (source + steps) % count) for source in range(count)]
    return lax.ppermute(value, axis, pairs)


def velocity_tables(node_count):
    pair_count = node_count * node_count
    spacing = 2.0 * node_reach / (node_count - 1)
    node_line = (np.arange(node_count, dtype=np.float64) - 0.5 * (node_count - 1)) * spacing
    grid_shape = (pair_count, node_count)
    along_x = np.broadcast_to(np.repeat(node_line, node_count)[:, None], grid_shape)
    along_y = np.broadcast_to(np.tile(node_line, node_count)[:, None], grid_shape)
    along_z = np.broadcast_to(node_line[None, :], grid_shape)
    square = along_x * along_x + along_y * along_y + along_z * along_z
    heat_term = square - 2.5
    functions = [
        np.ones(grid_shape),
        along_x,
        along_y,
        along_z,
        square - 1.5,
        along_x * along_y,
        along_x * along_z,
        along_y * along_z,
        along_x * along_x - along_y * along_y,
        along_y * along_y - along_z * along_z,
        along_x * heat_term,
        along_y * heat_term,
        along_z * heat_term,
    ]
    stacked = np.stack(functions)
    basis = stacked / np.sqrt(np.mean(stacked * stacked, axis=(1, 2), keepdims=True))
    weights = np.exp(-square) * (spacing * spacing * spacing) / math.pi**1.5
    recon = basis * weights[None]
    return node_line, basis, recon


def bf16_split(table, parts):
    rest = np.asarray(table, np.float64)
    pieces = []
    for _ in range(parts):
        piece = rest.astype(np.float32).astype(jnp.bfloat16).astype(np.float64)
        pieces.append(piece)
        rest = rest - piece
    return pieces


def on_device(cotangent, freq, ratio, coupling, wall, inlet, face_type):
    pair_count = cotangent.shape[1]
    node_count = cotangent.shape[2]
    cell_count = cotangent.shape[3]
    assert cell_count == NZ
    half = pair_count // 2
    moment_count = coupling.shape[2]
    species_count = lax.axis_size("species")

    node_line, basis, recon = velocity_tables(node_count)
    basis_k = np.transpose(basis, (0, 2, 1)).reshape(moment_count, node_count * pair_count)
    basis_parts = np.concatenate(bf16_split(basis_k, 3), axis=0)
    basis_parts = jnp.asarray(basis_parts.astype(jnp.bfloat16))
    weight_k = (recon[0] / basis[0]).T.reshape(-1).astype(np.float32)

    field_in = jnp.transpose(cotangent[0], (1, 0, 2))
    margin = (-half) % 16
    upper_in, lower_in = split_halves(field_in, half - margin, half + margin)
    got_next = passed_along(upper_in, "space", -1)
    got_prev = passed_along(lower_in, "space", 1)

    open_cells = (1 - wall).astype(jnp.float32)
    keep_upper = open_cells * (1.0 - inlet.astype(jnp.float32))
    upward = (jnp.arange(pair_count) >= half)[None, :, None]
    keep = jnp.where(upward, keep_upper[None, None, :], open_cells[None, None, :])
    masked = field_in * keep.astype(jnp.bfloat16)
    parts = jnp.dot(
        basis_parts,
        masked.reshape(node_count * pair_count, cell_count),
        preferred_element_type=jnp.float32,
    )
    moments = parts[:moment_count] + parts[moment_count : 2 * moment_count] + parts[2 * moment_count :]

    species_index = lax.axis_index("species")
    row_k = lax.dynamic_index_in_dim(coupling, species_index, axis=0, keepdims=False)
    own_weight = lax.dynamic_index_in_dim(row_k, species_index, axis=0, keepdims=False)
    cross = own_weight[:, None] * moments
    for shift in range(1, species_count):
        source = (species_index - shift) % species_count
        other = passed_along(moments, "species", shift)
        weight = lax.dynamic_index_in_dim(row_k, source, axis=0, keepdims=False)
        cross = cross + weight[:, None] * other

    rows = 16
    assert moment_count + 2 < rows
    packet = jnp.concatenate(
        [
            cross,
            open_cells[None],
            keep_upper[None],
            jnp.zeros((rows - moment_count - 2, cell_count), jnp.float32),
        ],
        axis=0,
    )
    packet_next = passed_along(packet, "space", -1)
    packet_prev = passed_along(packet, "space", 1)

    rate_value = freq[0]
    scale_factor = courant_max * ratio[0] / node_reach
    line = jnp.asarray(node_line.astype(np.float32))
    pair_line = jnp.repeat(line, node_count)
    adv_x = jnp.abs(scale_factor * pair_line)
    adv_z = jnp.abs(scale_factor * line)
    columns = jnp.broadcast_to(
        jnp.stack([1.0 - adv_x, adv_x])[:, :, None], (2, pair_count, cell_count)
    )
    scalars = jnp.concatenate(
        [adv_z, jnp.zeros((31 - node_count,), jnp.float32), (1.0 - rate_value)[None]]
    )
    faces = face_type[:, 0]

    lanes = 128
    recon_halves = jnp.asarray(packed_recon(recon, rows, lanes))

    flip_rows = lax.broadcasted_iota(jnp.int32, (pair_count, pair_count), 0)
    flip_cols = lax.broadcasted_iota(jnp.int32, (pair_count, pair_count), 1)
    flip = (flip_rows + flip_cols == pair_count - 1).astype(jnp.bfloat16)

    partial = own_kernel(field_in, recon_halves, packet, columns, flip, scalars, faces)
    out = halo_kernel(
        partial, got_next, got_prev, recon_halves, packet_next, packet_prev,
        columns, scalars,
    )
    return jnp.transpose(out, (1, 0, 2))[None]


def packed_recon(recon, rows, lanes):
    moment_count, pair_count, node_count = recon.shape
    half = pair_count // 2
    table = np.transpose(recon, (2, 1, 0))
    parts = bf16_split(table, 2)
    order = [0, 0, 1]
    packed = np.zeros((node_count, half, lanes), np.float32)
    for side in range(2):
        for block, part in enumerate(order):
            at = side * (lanes // 2) + block * rows
            packed[:, :, at : at + moment_count] = parts[part][:, side * half : (side + 1) * half]
    return packed.astype(jnp.bfloat16)


def split_halves(field_in, start, wide):
    node_count, pair_count, cell_count = field_in.shape
    group = 5 if node_count % 5 == 0 else 1

    def kernel(x_ref, up_ref, lo_ref):
        up_ref[...] = x_ref[:, start : start + wide, :]
        lo_ref[...] = x_ref[:, :wide, :]

    shape = jax.ShapeDtypeStruct((node_count, wide, cell_count), field_in.dtype)
    return pl.pallas_call(
        kernel,
        grid=(node_count // group,),
        in_specs=[pl.BlockSpec((group, pair_count, cell_count), lambda i: (i, 0, 0))],
        out_specs=[
            pl.BlockSpec((group, wide, cell_count), lambda i: (i, 0, 0)),
            pl.BlockSpec((group, wide, cell_count), lambda i: (i, 0, 0)),
        ],
        out_shape=[shape, shape],
        compiler_params=pltpu.CompilerParams(dimension_semantics=("arbitrary",)),
    )(field_in)


def cross_matrix(packet, moment_count, side):
    rows, cells = packet.shape
    row = lax.broadcasted_iota(jnp.int32, packet.shape, 0)
    values = jnp.where(row < moment_count, packet, 0.0)
    c1 = values.astype(jnp.bfloat16)
    c2 = (values - c1.astype(jnp.float32)).astype(jnp.bfloat16)
    gap = jnp.zeros((64 - 3 * rows, cells), jnp.bfloat16)
    lead = jnp.zeros((64, cells), jnp.bfloat16)
    pieces = [c1, c2, c1, gap]
    return jnp.concatenate([lead] + pieces if side else pieces + [lead], axis=0)


def own_kernel(field_in, recon_halves, packet, columns, flip, scalars, faces):
    node_count, pair_count, cell_count = field_in.shape
    half = pair_count // 2
    steps = node_count // 2
    moment_count = packet.shape[0] - 3
    group = 5 if steps % 5 == 0 else 1
    blocks = steps // group

    def kernel(sc_ref, face_ref, cot_lo, cot_hi, rec_lo, rec_hi, pk_ref, col_ref, flip_ref, out_ref):
        b = pl.program_id(0)
        row = lax.broadcasted_iota(jnp.int32, (pair_count, cell_count), 0)
        lane = lax.broadcasted_iota(jnp.int32, (pair_count, cell_count), 1)
        pk = pk_ref[...]
        rate = sc_ref[31]
        keep = rate * jnp.where(row >= half, pk[moment_count + 1 : moment_count + 2, :], pk[moment_count : moment_count + 1, :])
        own_both = jnp.concatenate(
            [cross_matrix(pk, moment_count, 0), cross_matrix(pk, moment_count, 1)], axis=1
        )
        base = col_ref[0]
        face_a = face_ref[0] == 1
        face_b = face_ref[1] == 1

        def relax(values, rec_ref, at):
            both = jnp.dot(rec_ref[at], own_both, preferred_element_type=jnp.float32)
            rebuilt = jnp.concatenate([both[:, :cell_count], both[:, cell_count:]], axis=0)
            return (keep * values.astype(jnp.float32) + rebuilt).astype(jnp.bfloat16)

        def one(t, carry):
            u = group - 1 - t
            j = b * group + t
            relaxed_a = relax(cot_lo[t], rec_lo, t)
            relaxed_b = relax(cot_hi[u], rec_hi, u)
            edges = jnp.where(lane == 0, relaxed_b, relaxed_a)
            flipped = jnp.dot(flip_ref[...], edges, preferred_element_type=jnp.float32)
            edges32 = edges.astype(jnp.float32)
            source_a = jnp.where(face_a, flipped, edges32)
            source_b = jnp.where(face_b, flipped, edges32)
            ra = relaxed_a.astype(jnp.float32)
            rb = relaxed_b.astype(jnp.float32)
            near_a = jnp.where(lane == 0, source_a, pltpu.roll(ra, 1, 1))
            near_b = jnp.where(lane == cell_count - 1, source_b, pltpu.roll(rb, cell_count - 1, 1))
            zw_a = sc_ref[j]
            zw_b = sc_ref[node_count - 1 - j]
            out_ref[0, t] = (base - zw_a) * ra + zw_a * near_a
            out_ref[1, t] = (base - zw_b) * rb + zw_b * near_b
            return carry

        lax.fori_loop(0, group, one, 0)

    block = (group, pair_count, cell_count)
    smem = pl.BlockSpec(memory_space=pltpu.SMEM)
    in_specs = [
        smem,
        smem,
        pl.BlockSpec(block, lambda b: (b, 0, 0)),
        pl.BlockSpec(block, lambda b: (2 * blocks - 1 - b, 0, 0)),
        pl.BlockSpec((group, half, recon_halves.shape[2]), lambda b: (b, 0, 0)),
        pl.BlockSpec((group, half, recon_halves.shape[2]), lambda b: (2 * blocks - 1 - b, 0, 0)),
        pl.BlockSpec(packet.shape, lambda b: (0, 0)),
        pl.BlockSpec((1, pair_count, cell_count), lambda b: (0, 0, 0)),
        pl.BlockSpec(flip.shape, lambda b: (0, 0)),
    ]
    return pl.pallas_call(
        kernel,
        grid=(blocks,),
        in_specs=in_specs,
        out_specs=pl.BlockSpec((2,) + block, lambda b: (0, b, 0, 0)),
        out_shape=jax.ShapeDtypeStruct((2, steps, pair_count, cell_count), jnp.float32),
        compiler_params=pltpu.CompilerParams(
            dimension_semantics=("arbitrary",), vmem_limit_bytes=48 * 1024 * 1024
        ),
    )(scalars, faces, field_in, field_in, recon_halves, recon_halves, packet, columns, flip)


def halo_kernel(partial, got_next, got_prev, recon_halves, packet_next, packet_prev, columns, scalars):
    node_count, wide, cell_count = got_next.shape
    half = recon_halves.shape[1]
    margin = wide - half
    pair_count = 2 * half
    steps = node_count // 2
    moment_count = packet_next.shape[0] - 3
    group = 5 if steps % 5 == 0 else 1
    blocks = node_count // group
    lower_blocks = steps // group

    def kernel(sc_ref, part_ref, nxt_ref, prv_ref, rec_ref, pn_ref, pp_ref, col_ref, out_ref):
        i = pl.program_id(0)
        rate = sc_ref[31]
        pn = pn_ref[...]
        pp = pp_ref[...]
        halo_mats = jnp.concatenate(
            [cross_matrix(pn, moment_count, 1), cross_matrix(pp, moment_count, 0)], axis=1
        )
        keep_up = rate * pn[moment_count + 1 : moment_count + 2, :]
        keep_down = rate * pp[moment_count : moment_count + 1, :]
        side = col_ref[0]

        def run(mirrored):
            def one(t, carry):
                both = jnp.dot(rec_ref[t], halo_mats, preferred_element_type=jnp.float32)
                up = both[:, :cell_count]
                down = both[:, cell_count:]
                nxt = nxt_ref[t].astype(jnp.float32)[margin:]
                prv = prv_ref[t].astype(jnp.float32)[:half]
                up = (keep_up * nxt + up).astype(jnp.bfloat16)
                down = (keep_down * prv + down).astype(jnp.bfloat16)
                shifted = jnp.concatenate([down.astype(jnp.float32), up.astype(jnp.float32)], axis=0)
                part = part_ref[0, group - 1 - t] if mirrored else part_ref[0, t]
                out_ref[t] = (part + side * shifted).astype(jnp.bfloat16)
                return carry

            lax.fori_loop(0, group, one, 0)

        @pl.when(i < lower_blocks)
        def _():
            run(False)

        @pl.when(i >= lower_blocks)
        def _():
            run(True)

    block = (group, pair_count, cell_count)
    smem = pl.BlockSpec(memory_space=pltpu.SMEM)
    in_specs = [
        smem,
        pl.BlockSpec(
            (1,) + block,
            lambda i: (
                jnp.where(i < lower_blocks, 0, 1),
                jnp.where(i < lower_blocks, i, blocks - 1 - i),
                0,
                0,
            ),
        ),
        pl.BlockSpec((group, wide, cell_count), lambda i: (i, 0, 0)),
        pl.BlockSpec((group, wide, cell_count), lambda i: (i, 0, 0)),
        pl.BlockSpec((group, half, recon_halves.shape[2]), lambda i: (i, 0, 0)),
        pl.BlockSpec(packet_next.shape, lambda i: (0, 0)),
        pl.BlockSpec(packet_prev.shape, lambda i: (0, 0)),
        pl.BlockSpec((1, pair_count, cell_count), lambda i: (1, 0, 0)),
    ]
    return pl.pallas_call(
        kernel,
        grid=(blocks,),
        in_specs=in_specs,
        out_specs=pl.BlockSpec(block, lambda i: (i, 0, 0)),
        out_shape=jax.ShapeDtypeStruct((node_count, pair_count, cell_count), jnp.bfloat16),
        compiler_params=pltpu.CompilerParams(
            dimension_semantics=("arbitrary",), vmem_limit_bytes=48 * 1024 * 1024
        ),
    )(scalars, partial, got_next, got_prev, recon_halves, packet_next, packet_prev, columns)


def solution(mesh):
    in_specs = (
        P("species", None, None, "space"),
        P("species"),
        P("species"),
        P(),
        P("space"),
        P("space"),
        P(None, "space"),
    )
    out_specs = P("species", None, None, "space")

    return jax.shard_map(on_device, mesh=mesh, in_specs=in_specs, out_specs=out_specs, check_vma=False)
```

```python
import math

import numpy as np
import jax
import jax.numpy as jnp
from jax import lax
from jax.experimental import pallas as pl
from jax.experimental.pallas import tpu as pltpu
from jax.sharding import PartitionSpec as P


NZ = 128

courant_max = 0.45
node_reach = 2.85


def passed_along(value, axis, steps):
    count = lax.axis_size(axis)
    pairs = [(source, (source + steps) % count) for source in range(count)]
    return lax.ppermute(value, axis, pairs)


def velocity_tables(node_count):
    pair_count = node_count * node_count
    spacing = 2.0 * node_reach / (node_count - 1)
    node_line = (np.arange(node_count, dtype=np.float64) - 0.5 * (node_count - 1)) * spacing
    grid_shape = (pair_count, node_count)
    along_x = np.broadcast_to(np.repeat(node_line, node_count)[:, None], grid_shape)
    along_y = np.broadcast_to(np.tile(node_line, node_count)[:, None], grid_shape)
    along_z = np.broadcast_to(node_line[None, :], grid_shape)
    square = along_x * along_x + along_y * along_y + along_z * along_z
    heat_term = square - 2.5
    functions = [
        np.ones(grid_shape),
        along_x,
        along_y,
        along_z,
        square - 1.5,
        along_x * along_y,
        along_x * along_z,
        along_y * along_z,
        along_x * along_x - along_y * along_y,
        along_y * along_y - along_z * along_z,
        along_x * heat_term,
        along_y * heat_term,
        along_z * heat_term,
    ]
    stacked = np.stack(functions)
    basis = stacked / np.sqrt(np.mean(stacked * stacked, axis=(1, 2), keepdims=True))
    weights = np.exp(-square) * (spacing * spacing * spacing) / math.pi**1.5
    recon = basis * weights[None]
    return node_line, basis, recon


def bf16_split(table, parts):
    rest = np.asarray(table, np.float64)
    pieces = []
    for _ in range(parts):
        piece = rest.astype(np.float32).astype(jnp.bfloat16).astype(np.float64)
        pieces.append(piece)
        rest = rest - piece
    return pieces


def on_device(cotangent, freq, ratio, coupling, wall, inlet, face_type):
    pair_count = cotangent.shape[1]
    node_count = cotangent.shape[2]
    cell_count = cotangent.shape[3]
    assert cell_count == NZ
    half = pair_count // 2
    moment_count = coupling.shape[2]
    species_count = lax.axis_size("species")

    node_line, basis, recon = velocity_tables(node_count)
    basis_k = np.transpose(basis, (0, 2, 1)).reshape(moment_count, node_count * pair_count)
    basis_parts = np.concatenate(bf16_split(basis_k, 3), axis=0)
    basis_parts = jnp.asarray(basis_parts.astype(jnp.bfloat16))
    weight_k = (recon[0] / basis[0]).T.reshape(-1).astype(np.float32)

    field_in = jnp.transpose(cotangent[0], (1, 0, 2))
    margin = 0
    upper_in = field_in[:, half - margin :, :]
    lower_in = field_in[:, : half + margin, :]
    got_next = passed_along(upper_in, "space", -1)
    got_prev = passed_along(lower_in, "space", 1)

    open_cells = (1 - wall).astype(jnp.float32)
    keep_upper = open_cells * (1.0 - inlet.astype(jnp.float32))
    upward = (jnp.arange(pair_count) >= half)[None, :, None]
    keep = jnp.where(upward, keep_upper[None, None, :], open_cells[None, None, :])
    masked = field_in * keep.astype(jnp.bfloat16)
    parts = jnp.dot(
        basis_parts,
        masked.reshape(node_count * pair_count, cell_count),
        preferred_element_type=jnp.float32,
    )
    moments = parts[:moment_count] + parts[moment_count : 2 * moment_count] + parts[2 * moment_count :]

    species_index = lax.axis_index("species")
    row_k = lax.dynamic_index_in_dim(coupling, species_index, axis=0, keepdims=False)
    own_weight = lax.dynamic_index_in_dim(row_k, species_index, axis=0, keepdims=False)
    cross = own_weight[:, None] * moments
    for shift in range(1, species_count):
        source = (species_index - shift) % species_count
        other = passed_along(moments, "species", shift)
        weight = lax.dynamic_index_in_dim(row_k, source, axis=0, keepdims=False)
        cross = cross + weight[:, None] * other

    rows = 16
    assert moment_count + 2 < rows
    packet = jnp.concatenate(
        [
            cross,
            open_cells[None],
            keep_upper[None],
            jnp.zeros((rows - moment_count - 2, cell_count), jnp.float32),
        ],
        axis=0,
    )
    packet_next = passed_along(packet, "space", -1)
    packet_prev = passed_along(packet, "space", 1)

    rate_value = freq[0]
    scale_factor = courant_max * ratio[0] / node_reach
    line = jnp.asarray(node_line.astype(np.float32))
    pair_line = jnp.repeat(line, node_count)
    adv_x = jnp.abs(scale_factor * pair_line)
    adv_z = jnp.abs(scale_factor * line)
    columns = jnp.broadcast_to(
        jnp.stack([1.0 - adv_x, adv_x])[:, :, None], (2, pair_count, cell_count)
    )
    scalars = jnp.concatenate(
        [adv_z, jnp.zeros((31 - node_count,), jnp.float32), (1.0 - rate_value)[None]]
    )
    faces = face_type[:, 0]

    lanes = 128
    recon_halves = jnp.asarray(packed_recon(recon, rows, lanes))

    flip_rows = lax.broadcasted_iota(jnp.int32, (pair_count, pair_count), 0)
    flip_cols = lax.broadcasted_iota(jnp.int32, (pair_count, pair_count), 1)
    flip = (flip_rows + flip_cols == pair_count - 1).astype(jnp.bfloat16)

    partial = own_kernel(field_in, recon_halves, packet, flip, freq, ratio, faces)
    out = halo_kernel(partial, got_next, got_prev, recon_halves, packet_next, packet_prev, freq, ratio)
    return jnp.transpose(out, (1, 0, 2))[None]


def packed_recon(recon, rows, lanes):
    moment_count, pair_count, node_count = recon.shape
    half = pair_count // 2
    table = np.transpose(recon, (2, 1, 0))
    parts = bf16_split(table, 2)
    order = [0, 0, 1]
    packed = np.zeros((node_count, half, lanes), np.float32)
    for side in range(2):
        for block, part in enumerate(order):
            at = side * (lanes // 2) + block * rows
            packed[:, :, at : at + moment_count] = parts[part][:, side * half : (side + 1) * half]
    return packed.astype(jnp.bfloat16)


def cross_matrix(packet, moment_count, side):
    rows, cells = packet.shape
    row = lax.broadcasted_iota(jnp.int32, packet.shape, 0)
    values = jnp.where(row < moment_count, packet, 0.0)
    c1 = values.astype(jnp.bfloat16)
    c2 = (values - c1.astype(jnp.float32)).astype(jnp.bfloat16)
    gap = jnp.zeros((64 - 3 * rows, cells), jnp.bfloat16)
    lead = jnp.zeros((64, cells), jnp.bfloat16)
    pieces = [c1, c2, c1, gap]
    return jnp.concatenate([lead] + pieces if side else pieces + [lead], axis=0)


def coefficients(ratio_ref, pair_count, node_count, cell_count):
    spacing = 2.0 * node_reach / (node_count - 1)
    speed = jnp.full((1, cell_count), ratio_ref[0], jnp.float32)
    scale = courant_max * speed / node_reach
    row = lax.broadcasted_iota(jnp.int32, (pair_count, cell_count), 0).astype(jnp.float32)
    ix = jnp.floor((row + 0.5) * (1.0 / node_count))
    ux = (ix - 0.5 * (node_count - 1)) * spacing
    return scale, jnp.abs(scale * ux)


def z_weight(scale, iz, node_count, cell_count):
    spacing = 2.0 * node_reach / (node_count - 1)
    at = jnp.full((1, cell_count), iz, jnp.int32).astype(jnp.float32)
    return jnp.abs(scale * ((at - 0.5 * (node_count - 1)) * spacing))


def own_kernel(field_in, recon_halves, packet, flip, freq, ratio, faces):
    node_count, pair_count, cell_count = field_in.shape
    half = pair_count // 2
    steps = node_count // 2
    moment_count = packet.shape[0] - 3
    group = 5 if steps % 5 == 0 else 1
    blocks = steps // group

    def kernel(freq_ref, ratio_ref, face_ref, cot_lo, cot_hi, rec_lo, rec_hi, pk_ref, flip_ref, out_ref):
        b = pl.program_id(0)
        row = lax.broadcasted_iota(jnp.int32, (pair_count, cell_count), 0)
        lane = lax.broadcasted_iota(jnp.int32, (pair_count, cell_count), 1)
        pk = pk_ref[...]
        rate = 1.0 - freq_ref[0]
        keep = rate * jnp.where(row >= half, pk[moment_count + 1 : moment_count + 2, :], pk[moment_count : moment_count + 1, :])
        own_both = jnp.concatenate(
            [cross_matrix(pk, moment_count, 0), cross_matrix(pk, moment_count, 1)], axis=1
        )
        scale, side = coefficients(ratio_ref, pair_count, node_count, cell_count)
        base = 1.0 - side
        face_a = face_ref[0] == 1
        face_b = face_ref[1] == 1

        def relax(values, rec_ref, at):
            both = jnp.dot(rec_ref[at], own_both, preferred_element_type=jnp.float32)
            rebuilt = jnp.concatenate([both[:, :cell_count], both[:, cell_count:]], axis=0)
            return (keep * values.astype(jnp.float32) + rebuilt).astype(jnp.bfloat16)

        def one(t, carry):
            u = group - 1 - t
            j = b * group + t
            relaxed_a = relax(cot_lo[t], rec_lo, t)
            relaxed_b = relax(cot_hi[u], rec_hi, u)
            edges = jnp.where(lane == 0, relaxed_b, relaxed_a)
            flipped = jnp.dot(flip_ref[...], edges, preferred_element_type=jnp.float32)
            edges32 = edges.astype(jnp.float32)
            source_a = jnp.where(face_a, flipped, edges32)
            source_b = jnp.where(face_b, flipped, edges32)
            ra = relaxed_a.astype(jnp.float32)
            rb = relaxed_b.astype(jnp.float32)
            near_a = jnp.where(lane == 0, source_a, pltpu.roll(ra, 1, 1))
            near_b = jnp.where(lane == cell_count - 1, source_b, pltpu.roll(rb, cell_count - 1, 1))
            zw_a = z_weight(scale, j, node_count, cell_count)
            zw_b = z_weight(scale, node_count - 1 - j, node_count, cell_count)
            out_ref[0, t] = (base - zw_a) * ra + zw_a * near_a
            out_ref[1, t] = (base - zw_b) * rb + zw_b * near_b
            return carry

        lax.fori_loop(0, group, one, 0)

    block = (group, pair_count, cell_count)
    smem = pl.BlockSpec(memory_space=pltpu.SMEM)
    in_specs = [
        smem,
        smem,
        smem,
        pl.BlockSpec(block, lambda b: (b, 0, 0)),
        pl.BlockSpec(block, lambda b: (2 * blocks - 1 - b, 0, 0)),
        pl.BlockSpec((group, half, recon_halves.shape[2]), lambda b: (b, 0, 0)),
        pl.BlockSpec((group, half, recon_halves.shape[2]), lambda b: (2 * blocks - 1 - b, 0, 0)),
        pl.BlockSpec(packet.shape, lambda b: (0, 0)),
        pl.BlockSpec(flip.shape, lambda b: (0, 0)),
    ]
    return pl.pallas_call(
        kernel,
        grid=(blocks,),
        in_specs=in_specs,
        out_specs=pl.BlockSpec((2,) + block, lambda b: (0, b, 0, 0)),
        out_shape=jax.ShapeDtypeStruct((2, steps, pair_count, cell_count), jnp.float32),
        compiler_params=pltpu.CompilerParams(
            dimension_semantics=("arbitrary",), vmem_limit_bytes=48 * 1024 * 1024
        ),
    )(freq, ratio, faces, field_in, field_in, recon_halves, recon_halves, packet, flip)


def halo_kernel(partial, got_next, got_prev, recon_halves, packet_next, packet_prev, freq, ratio):
    node_count, wide, cell_count = got_next.shape
    half = recon_halves.shape[1]
    margin = wide - half
    pair_count = 2 * half
    steps = node_count // 2
    moment_count = packet_next.shape[0] - 3
    group = 5 if steps % 5 == 0 else 1
    blocks = node_count // group
    lower_blocks = steps // group

    def kernel(freq_ref, ratio_ref, part_ref, nxt_ref, prv_ref, rec_ref, pn_ref, pp_ref, out_ref):
        i = pl.program_id(0)
        rate = 1.0 - freq_ref[0]
        pn = pn_ref[...]
        pp = pp_ref[...]
        halo_mats = jnp.concatenate(
            [cross_matrix(pn, moment_count, 1), cross_matrix(pp, moment_count, 0)], axis=1
        )
        keep_up = rate * pn[moment_count + 1 : moment_count + 2, :]
        keep_down = rate * pp[moment_count : moment_count + 1, :]
        side = coefficients(ratio_ref, pair_count, node_count, cell_count)[1]

        def run(mirrored):
            def one(t, carry):
                both = jnp.dot(rec_ref[t], halo_mats, preferred_element_type=jnp.float32)
                up = both[:, :cell_count]
                down = both[:, cell_count:]
                nxt = nxt_ref[t].astype(jnp.float32)[margin:]
                prv = prv_ref[t].astype(jnp.float32)[:half]
                up = (keep_up * nxt + up).astype(jnp.bfloat16)
                down = (keep_down * prv + down).astype(jnp.bfloat16)
                shifted = jnp.concatenate([down.astype(jnp.float32), up.astype(jnp.float32)], axis=0)
                part = part_ref[0, group - 1 - t] if mirrored else part_ref[0, t]
                out_ref[t] = (part + side * shifted).astype(jnp.bfloat16)
                return carry

            lax.fori_loop(0, group, one, 0)

        @pl.when(i < lower_blocks)
        def _():
            run(False)

        @pl.when(i >= lower_blocks)
        def _():
            run(True)

    block = (group, pair_count, cell_count)
    smem = pl.BlockSpec(memory_space=pltpu.SMEM)
    in_specs = [
        smem,
        smem,
        pl.BlockSpec(
            (1,) + block,
            lambda i: (
                jnp.where(i < lower_blocks, 0, 1),
                jnp.where(i < lower_blocks, i, blocks - 1 - i),
                0,
                0,
            ),
        ),
        pl.BlockSpec((group, wide, cell_count), lambda i: (i, 0, 0)),
        pl.BlockSpec((group, wide, cell_count), lambda i: (i, 0, 0)),
        pl.BlockSpec((group, half, recon_halves.shape[2]), lambda i: (i, 0, 0)),
        pl.BlockSpec(packet_next.shape, lambda i: (0, 0)),
        pl.BlockSpec(packet_prev.shape, lambda i: (0, 0)),
    ]
    return pl.pallas_call(
        kernel,
        grid=(blocks,),
        in_specs=in_specs,
        out_specs=pl.BlockSpec(block, lambda i: (i, 0, 0)),
        out_shape=jax.ShapeDtypeStruct((node_count, pair_count, cell_count), jnp.bfloat16),
        compiler_params=pltpu.CompilerParams(
            dimension_semantics=("arbitrary",), vmem_limit_bytes=48 * 1024 * 1024
        ),
    )(freq, ratio, partial, got_next, got_prev, recon_halves, packet_next, packet_prev)


def solution(mesh):
    in_specs = (
        P("species", None, None, "space"),
        P("species"),
        P("species"),
        P(),
        P("space"),
        P("space"),
        P(None, "space"),
    )
    out_specs = P("species", None, None, "space")

    return jax.shard_map(on_device, mesh=mesh, in_specs=in_specs, out_specs=out_specs, check_vma=False)
```
